32 devices in a mesh: mem: 4 (over z), tile: 8 (over y, x, core).
Axes of the slice: x: 2, y: 2, z: 4, core: 2. Of those that a mesh axis runs over, the one named last changes fastest.
Arguments:
- source_blocks: bfloat16 [1024, 8, 2, 256], P('tile', 'mem'), may hold values from -6 to 6
- send_blocks: int32 [8, 8, 24], P('tile'), may hold values from 0 to 127
- recv_slot: int32 [8, 8, 24], P('tile'), may hold values from 0 to 95
- recv_weight: float32 [8, 8, 24], P('tile'), may hold values from 0.25 to 2
- recv_count: int32 [8, 8], P('tile'), may hold values from 0 to 24, as said below
- regional: bfloat16 [8, 2, 512, 384], P('mem', None, 'tile'), may hold values from -6 to 6
- x_operator: bfloat16 [512, 512], P(('mem', 'tile'))
- y_operator: bfloat16 [384, 384], P(('mem', 'tile'))
Outputs:
- blended: bfloat16 [8, 2, 512, 384], P('mem', None, 'tile')
The draws below stay inside these ranges and needn't reach their ends.
Inputs may be any that keep to these rules, and one draw needn't show every extreme that they name: `recv_count`: live entries of one pair of tiles number at most 24; some pairs in every draw have 24.
All inputs are finite; a program needn't handle non-finite values.
Results may differ from the reference program's by a relative error of at most 0.0055.
Values may be sent and summed in bfloat16 or wider, within the bound.
No kernel may reach another device: no remote copies, remote signals or barrier semaphores. Data moves between devices by JAX's collectives and lax.ppermute only.
A program may use at most 128 MiB of HBM per device.

```python
import math
import jax
import jax.numpy as jnp
from jax import lax

LEV = 2
SRC_DEV = 128
BS = 16
CX = 64
TILES = 8
MEMBERS = 8
NX = 512
NY = 384
NSRC = 1024
SLOTS = 96
CAP = 24


def line_operator(key, count):
    rows_index = jnp.arange(count)[:, None]
    cols_index = jnp.arange(count)[None, :]
    distance = jnp.abs(rows_index - cols_index).astype(jnp.float32)
    reach = count / 3.0
    noise = jax.random.truncated_normal(key, -3.0, 3.0, (count, count), jnp.float32)
    kernel = jnp.exp(-distance / reach) * (0.8 / reach + 0.6 * noise / math.sqrt(reach))
    return (kernel + jnp.where(rows_index == cols_index, 0.6, 0.0)).astype(jnp.bfloat16)


def draw_x_operator(key, part):
    return line_operator(jax.random.fold_in(key, 11), NX)


def draw_y_operator(key, part):
    return line_operator(jax.random.fold_in(key, 13), NY)


def draw_recv_count(key, part):
    window_start = jax.random.randint(jax.random.fold_in(key, 1), (), 0, TILES)
    others = jax.random.randint(jax.random.fold_in(key, 2), (TILES, TILES), 0, CAP // 2 + 1)
    source_index = jnp.arange(TILES, dtype=jnp.int32)[None, :]
    in_window = (source_index - window_start) % TILES < max(1, TILES // 4)
    return jnp.where(in_window, CAP, others).astype(jnp.int32)


def plant(result, key, smallest, top_value):
    dims = result.shape
    spot = [jax.random.randint(jax.random.fold_in(key, axis), (), 0, dims[axis]) for axis in range(len(dims))]
    result = result.at[tuple(spot)].set(smallest)
    longest = dims.index(max(dims))
    spot[longest] = (spot[longest] + 1) % dims[longest]
    return result.at[tuple(spot)].set(top_value)


def levels(stream_key, extent, shards, smallest, top_value):
    def one(dim, shards_of):
        heights = jax.random.uniform(jax.random.fold_in(jax.random.fold_in(stream_key, 6), dim), (shards_of,), jnp.float32, smallest / len(shards), top_value / len(shards))
        return jnp.repeat(jnp.exp(heights), extent[dim] // shards_of).reshape((-1,) + (1,) * (len(extent) - dim - 1))

    factor_of = one(*shards[0])
    for cut in shards[1:]:
        factor_of = factor_of * one(*cut)
    return factor_of


def bell_draw(stream_key, shape, spread, most, cuts=(), kind=jnp.bfloat16):
    array = spread * jax.random.normal(stream_key, shape, jnp.float32)
    if cuts:
        array = array * levels(stream_key, shape, cuts, -0.22, 0.18)
    return jnp.clip(array, -most, most).astype(kind)


def setup_inputs(seed: int = 0) -> dict:
    arg_keys = jax.random.split(jax.random.key(seed), 9)
    source_blocks = bell_draw(arg_keys[0], (NSRC, MEMBERS, LEV, BS * BS), 1.0, 6.0, ((0, 8), (1, 4)))
    send_blocks = plant(jax.random.randint(arg_keys[1], (TILES, TILES, CAP), 0, SRC_DEV), jax.random.fold_in(arg_keys[1], 1), 0, SRC_DEV - 1).astype(jnp.int32)
    recv_slot = plant(jax.random.randint(arg_keys[2], (TILES, TILES, CAP), 0, SLOTS), jax.random.fold_in(arg_keys[2], 1), 0, SLOTS - 1).astype(jnp.int32)
    recv_weight = jnp.clip(jnp.exp(math.log(2.0) - 2.0794415 * jax.random.uniform(arg_keys[3], (TILES, TILES, CAP), jnp.float32) ** levels(arg_keys[3], (TILES, TILES, CAP), ((0, 8),), -0.2, 0.2)), 0.25, 2.0)
    recv_count = draw_recv_count(jax.random.fold_in(arg_keys[8], 71), 0)
    regional = bell_draw(arg_keys[5], (MEMBERS, LEV, NX, NY), 1.0, 6.0, ((0, 4), (2, 8)))
    x_operator = draw_x_operator(jax.random.fold_in(arg_keys[8], 71), 0)
    y_operator = draw_y_operator(jax.random.fold_in(arg_keys[8], 71), 0)
    return {"source_blocks": source_blocks, "send_blocks": send_blocks, "recv_slot": recv_slot, "recv_weight": recv_weight, "recv_count": recv_count, "regional": regional, "x_operator": x_operator, "y_operator": y_operator}


def reference(source_blocks, send_blocks, recv_slot, recv_weight, recv_count, regional, x_operator, y_operator):
    def remap_tile(tile_index):
        picked = jnp.arange(TILES, dtype=jnp.int32)[:, None] * SRC_DEV + send_blocks[:, tile_index, :]
        arrived = jnp.take(source_blocks, picked.reshape(-1), axis=0)
        live_mask = lax.broadcasted_iota(jnp.int32, (TILES, CAP), 1) < recv_count[tile_index][:, None]
        weights = jnp.where(live_mask, recv_weight[tile_index], jnp.zeros((TILES, CAP), recv_weight.dtype)).reshape(-1)
        slot_match = recv_slot[tile_index].reshape(-1)[None, :] == lax.broadcasted_iota(jnp.int32, (SLOTS, TILES * CAP), 0)
        remap_weights = jnp.where(slot_match, weights[None, :], jnp.zeros((SLOTS, TILES * CAP), weights.dtype)).astype(jnp.bfloat16)
        remapped = jnp.dot(remap_weights, arrived.reshape(TILES * CAP, -1), preferred_element_type=jnp.float32)
        remapped = remapped.reshape(CX // BS, NY // BS, MEMBERS, LEV, BS, BS).transpose(2, 3, 0, 4, 1, 5).reshape(MEMBERS, LEV, CX, NY)
        local_regional = lax.dynamic_slice_in_dim(regional, (tile_index * CX).astype(jnp.int32), CX, 2)
        return (remapped - local_regional.astype(jnp.float32)).astype(jnp.bfloat16)

    pieces = lax.map(remap_tile, jnp.arange(TILES, dtype=jnp.int32))
    difference = pieces.transpose(1, 2, 0, 3, 4).reshape(MEMBERS, LEV, NX, NY)

    def filter_member(pair):
        diff_member, regional_member = pair
        after_first = jnp.einsum("ax,lxy->lay", x_operator.astype(jnp.float32), diff_member.astype(jnp.float32)).astype(jnp.bfloat16)
        after_second = jnp.einsum("by,lxy->lxb", y_operator.astype(jnp.float32), after_first.astype(jnp.float32))
        return (regional_member.astype(jnp.float32) + after_second).astype(jnp.bfloat16)

    return lax.map(filter_member, (difference, regional))
```

```python
import math

import jax
import jax.numpy as jnp
from jax import lax
from jax.sharding import PartitionSpec as P


def gather_rows(shard, axis_name):
    count = lax.axis_size(axis_name)
    copies = jnp.broadcast_to(shard[None], (count,) + shard.shape)
    return lax.all_to_all(copies, axis_name, split_axis=0, concat_axis=0, tiled=True)


def gather_operators(x_operator, y_operator):
    mem_count = lax.axis_size("mem")
    tile_count = lax.axis_size("tile")
    x_rows, x_cols = x_operator.shape
    y_rows, y_cols = y_operator.shape
    x_size = x_rows * x_cols
    both = jnp.concatenate([x_operator.reshape(-1), y_operator.reshape(-1)])
    both = gather_rows(gather_rows(both[None], "mem"), "tile")
    both = both.reshape(tile_count, mem_count, -1).transpose(1, 0, 2)
    x_full = both[:, :, :x_size].reshape(mem_count * tile_count * x_rows, x_cols)
    y_full = both[:, :, x_size:].reshape(mem_count * tile_count * y_rows, y_cols)
    return x_full, y_full


def body(
    source_blocks, send_blocks, recv_slot, recv_weight, recv_count, regional, x_operator, y_operator
):
    tile_count = lax.axis_size("tile")
    member_count, level_count, columns, y_cells = regional.shape
    capacity = send_blocks.shape[2]
    block_cells = source_blocks.shape[3]
    block_side = math.isqrt(block_cells)
    x_full, y_full = gather_operators(x_operator, y_operator)
    picked = send_blocks[0].reshape(-1)
    packed = jnp.take(source_blocks, picked, axis=0).reshape(
        tile_count, capacity, member_count, level_count, block_cells
    )
    arrived = lax.all_to_all(packed, "tile", split_axis=0, concat_axis=0, tiled=True)
    slot_count = columns // block_side * (y_cells // block_side)
    live_mask = lax.broadcasted_iota(jnp.int32, (tile_count, capacity), 1) < recv_count[0][:, None]
    weights = jnp.where(live_mask, recv_weight[0], 0.0).reshape(-1)
    slot_match = recv_slot[0].reshape(-1)[None, :] == lax.broadcasted_iota(
        jnp.int32, (slot_count, tile_count * capacity), 0
    )
    remap_weights = jnp.where(slot_match, weights[None, :], 0.0).astype(jnp.bfloat16)
    remapped = jnp.dot(
        remap_weights,
        arrived.reshape(tile_count * capacity, -1),
        preferred_element_type=jnp.float32,
    )
    remapped = remapped.reshape(
        columns // block_side,
        y_cells // block_side,
        member_count,
        level_count,
        block_side,
        block_side,
    )
    remapped = remapped.transpose(2, 3, 0, 4, 1, 5).reshape(
        member_count, level_count, columns, y_cells
    )
    difference = (remapped - regional.astype(jnp.float32)).astype(jnp.bfloat16)
    x_lines = lax.all_to_all(difference, "tile", split_axis=3, concat_axis=2, tiled=True)
    after_first = jnp.einsum(
        "ax,mlxy->mlay",
        x_full,
        x_lines,
        preferred_element_type=jnp.float32,
    ).astype(jnp.bfloat16)
    tile_back = lax.all_to_all(after_first, "tile", split_axis=2, concat_axis=3, tiled=True)
    after_second = jnp.einsum(
        "by,mlxy->mlxb",
        y_full,
        tile_back,
        preferred_element_type=jnp.float32,
    )
    return (regional.astype(jnp.float32) + after_second).astype(jnp.bfloat16)


def solution(mesh):
    placed = (
        P("tile", "mem", None, None),
        P("tile", None, None),
        P("tile", None, None),
        P("tile", None, None),
        P("tile", None),
        P("mem", None, "tile", None),
        P(("mem", "tile"), None),
        P(("mem", "tile"), None),
    )
    return jax.shard_map(
        body, mesh=mesh, in_specs=placed, out_specs=P("mem", None, "tile", None), check_vma=False
    )
```

```python
import math

import jax
import jax.numpy as jnp
from jax import lax
from jax.sharding import PartitionSpec as P


def gather_rows(shard, axis_name):
    count = lax.axis_size(axis_name)
    copies = jnp.broadcast_to(shard[None], (count,) + shard.shape)
    return lax.all_to_all(copies, axis_name, split_axis=0, concat_axis=0, tiled=True)


def exchange(data, extra):
    tile_count = data.shape[0]
    flat = data.reshape(tile_count, -1)
    size = flat.shape[1]
    payload = jnp.concatenate(
        [flat, jnp.broadcast_to(extra[None], (tile_count,) + extra.shape)], axis=1
    )
    got = lax.all_to_all(payload, "tile", split_axis=0, concat_axis=0, tiled=True)
    return got[:, :size].reshape(data.shape), got[:, size:]


def rows_in_order(got, rows, cols):
    tile_count, mem_count = got.shape[0], got.shape[1]
    return got.reshape(tile_count, mem_count, rows, cols).transpose(1, 0, 2, 3).reshape(
        mem_count * tile_count * rows, cols
    )


def body(
    source_blocks, send_blocks, recv_slot, recv_weight, recv_count, regional, x_operator, y_operator
):
    tile_count = lax.axis_size("tile")
    mem_count = lax.axis_size("mem")
    member_count, level_count, columns, y_cells = regional.shape
    capacity = send_blocks.shape[2]
    block_cells = source_blocks.shape[3]
    block_side = math.isqrt(block_cells)
    x_rows, x_cols = x_operator.shape
    y_rows, y_cols = y_operator.shape
    x_size = x_rows * x_cols

    both = jnp.concatenate([x_operator.reshape(-1), y_operator.reshape(-1)])
    both = gather_rows(both[None], "mem").reshape(mem_count, -1)
    x_part = both[:, :x_size].reshape(-1)
    y_part = both[:, x_size:].reshape(-1)

    picked = send_blocks[0].reshape(-1)
    packed = jnp.take(source_blocks, picked, axis=0).reshape(
        tile_count, capacity, member_count, level_count, block_cells
    )
    arrived = lax.all_to_all(packed, "tile", split_axis=0, concat_axis=0, tiled=True)
    slot_count = columns // block_side * (y_cells // block_side)
    live_mask = lax.broadcasted_iota(jnp.int32, (tile_count, capacity), 1) < recv_count[0][:, None]
    weights = jnp.where(live_mask, recv_weight[0], 0.0).reshape(-1)
    slot_match = recv_slot[0].reshape(-1)[None, :] == lax.broadcasted_iota(
        jnp.int32, (slot_count, tile_count * capacity), 0
    )
    remap_weights = jnp.where(slot_match, weights[None, :], 0.0).astype(jnp.bfloat16)
    remapped = jnp.dot(
        remap_weights,
        arrived.reshape(tile_count * capacity, -1),
        preferred_element_type=jnp.float32,
    )
    remapped = remapped.reshape(
        columns // block_side,
        y_cells // block_side,
        member_count,
        level_count,
        block_side,
        block_side,
    )
    remapped = remapped.transpose(2, 3, 0, 4, 1, 5).reshape(
        member_count, level_count, columns, y_cells
    )
    difference = (remapped - regional.astype(jnp.float32)).astype(jnp.bfloat16)

    y_chunk = y_cells // tile_count
    outgoing = difference.reshape(member_count, level_count, columns, tile_count, y_chunk)
    got, x_got = exchange(outgoing.transpose(3, 0, 1, 2, 4), x_part)
    x_lines = got.transpose(1, 2, 0, 3, 4).reshape(
        member_count, level_count, tile_count * columns, y_chunk
    )
    x_full = rows_in_order(x_got.reshape(tile_count, mem_count, -1), x_rows, x_cols)
    after_first = jnp.einsum(
        "ax,mlxy->mlay", x_full, x_lines, preferred_element_type=jnp.float32
    ).astype(jnp.bfloat16)

    back = after_first.reshape(member_count, level_count, tile_count, columns, y_chunk)
    got, y_got = exchange(back.transpose(2, 0, 1, 3, 4), y_part)
    tile_back = got.transpose(1, 2, 3, 0, 4).reshape(member_count, level_count, columns, y_cells)
    y_full = rows_in_order(y_got.reshape(tile_count, mem_count, -1), y_rows, y_cols)
    after_second = jnp.einsum(
        "by,mlxy->mlxb", y_full, tile_back, preferred_element_type=jnp.float32
    )
    return (regional.astype(jnp.float32) + after_second).astype(jnp.bfloat16)


def solution(mesh):
    placed = (
        P("tile", "mem", None, None),
        P("tile", None, None),
        P("tile", None, None),
        P("tile", None, None),
        P("tile", None),
        P("mem", None, "tile", None),
        P(("mem", "tile"), None),
        P(("mem", "tile"), None),
    )
    return jax.shard_map(
        body, mesh=mesh, in_specs=placed, out_specs=P("mem", None, "tile", None), check_vma=False
    )
```

```python
import math

import jax
import jax.numpy as jnp
from jax import lax
from jax.sharding import PartitionSpec as P


def doubling_gather(data, axis_name, bits):
    count = lax.axis_size(axis_name)
    index = lax.axis_index(axis_name)
    for bit in bits:
        received = lax.ppermute(data, axis_name, [(j, j ^ bit) for j in range(count)])
        high = (index // bit) % 2 == 1
        data = jnp.stack([jnp.where(high, received, data), jnp.where(high, data, received)])
    return data


def bit_order(count, bits):
    stacked = list(reversed(bits))
    return [stacked.index(bit) for bit in sorted(bits, reverse=True)]


def gather_operators(x_operator, y_operator):
    mem_count = lax.axis_size("mem")
    tile_count = lax.axis_size("tile")
    x_rows, x_cols = x_operator.shape
    y_rows, y_cols = y_operator.shape
    x_size = x_rows * x_cols
    both = jnp.concatenate([x_operator.reshape(-1), y_operator.reshape(-1)])
    mem_bits = [1 << k for k in range(mem_count.bit_length() - 1)]
    tile_bits = [1 << k for k in range(1, tile_count.bit_length() - 1)] + [1]
    both = doubling_gather(both, "mem", mem_bits)
    both = doubling_gather(both, "tile", tile_bits)
    tile_axes = bit_order(tile_count, tile_bits)
    mem_axes = [len(tile_bits) + k for k in bit_order(mem_count, mem_bits)]
    both = both.transpose(mem_axes + tile_axes + [both.ndim - 1]).reshape(
        mem_count * tile_count, -1
    )
    x_full = both[:, :x_size].reshape(mem_count * tile_count * x_rows, x_cols)
    y_full = both[:, x_size:].reshape(mem_count * tile_count * y_rows, y_cols)
    return x_full, y_full


def body(
    source_blocks, send_blocks, recv_slot, recv_weight, recv_count, regional, x_operator, y_operator
):
    tile_count = lax.axis_size("tile")
    member_count, level_count, columns, y_cells = regional.shape
    capacity = send_blocks.shape[2]
    block_cells = source_blocks.shape[3]
    block_side = math.isqrt(block_cells)
    x_full, y_full = gather_operators(x_operator, y_operator)
    picked = send_blocks[0].reshape(-1)
    packed = jnp.take(source_blocks, picked, axis=0).reshape(
        tile_count, capacity, member_count, level_count, block_cells
    )
    arrived = lax.all_to_all(packed, "tile", split_axis=0, concat_axis=0, tiled=True)
    slot_count = columns // block_side * (y_cells // block_side)
    live_mask = lax.broadcasted_iota(jnp.int32, (tile_count, capacity), 1) < recv_count[0][:, None]
    weights = jnp.where(live_mask, recv_weight[0], 0.0).reshape(-1)
    slot_match = recv_slot[0].reshape(-1)[None, :] == lax.broadcasted_iota(
        jnp.int32, (slot_count, tile_count * capacity), 0
    )
    remap_weights = jnp.where(slot_match, weights[None, :], 0.0).astype(jnp.bfloat16)
    remapped = jnp.dot(
        remap_weights,
        arrived.reshape(tile_count * capacity, -1),
        preferred_element_type=jnp.float32,
    )
    remapped = remapped.reshape(
        columns // block_side,
        y_cells // block_side,
        member_count,
        level_count,
        block_side,
        block_side,
    )
    remapped = remapped.transpose(2, 3, 0, 4, 1, 5).reshape(
        member_count, level_count, columns, y_cells
    )
    difference = (remapped - regional.astype(jnp.float32)).astype(jnp.bfloat16)
    x_lines = lax.all_to_all(difference, "tile", split_axis=3, concat_axis=2, tiled=True)
    after_first = jnp.einsum(
        "ax,mlxy->mlay",
        x_full,
        x_lines,
        preferred_element_type=jnp.float32,
    ).astype(jnp.bfloat16)
    tile_back = lax.all_to_all(after_first, "tile", split_axis=2, concat_axis=3, tiled=True)
    after_second = jnp.einsum(
        "by,mlxy->mlxb",
        y_full,
        tile_back,
        preferred_element_type=jnp.float32,
    )
    return (regional.astype(jnp.float32) + after_second).astype(jnp.bfloat16)


def solution(mesh):
    placed = (
        P("tile", "mem", None, None),
        P("tile", None, None),
        P("tile", None, None),
        P("tile", None, None),
        P("tile", None),
        P("mem", None, "tile", None),
        P(("mem", "tile"), None),
        P(("mem", "tile"), None),
    )
    return jax.shard_map(
        body, mesh=mesh, in_specs=placed, out_specs=P("mem", None, "tile", None), check_vma=False
    )
```

```python
import math

import jax
import jax.numpy as jnp
from jax import lax
from jax.sharding import PartitionSpec as P


def doubling_gather(data, axis_name, bits):
    count = lax.axis_size(axis_name)
    index = lax.axis_index(axis_name)
    for bit in bits:
        received = lax.ppermute(data, axis_name, [(j, j ^ bit) for j in range(count)])
        high = (index // bit) % 2 == 1
        data = jnp.stack([jnp.where(high, received, data), jnp.where(high, data, received)])
    return data


def bit_order(count, bits):
    stacked = list(reversed(bits))
    return [stacked.index(bit) for bit in sorted(bits, reverse=True)]


def gather_operators(x_operator, y_operator, after):
    mem_count = lax.axis_size("mem")
    tile_count = lax.axis_size("tile")
    x_rows, x_cols = x_operator.shape
    y_rows, y_cols = y_operator.shape
    x_size = x_rows * x_cols
    both = jnp.concatenate([x_operator.reshape(-1), y_operator.reshape(-1)])
    mem_bits = [1 << k for k in range(mem_count.bit_length() - 1)]
    tile_bits = [1 << k for k in range(1, tile_count.bit_length() - 1)] + [1]
    both = doubling_gather(both, "mem", mem_bits)
    both, after = lax.optimization_barrier((both, after))
    both = doubling_gather(both, "tile", tile_bits)
    tile_axes = bit_order(tile_count, tile_bits)
    mem_axes = [len(tile_bits) + k for k in bit_order(mem_count, mem_bits)]
    both = both.transpose(mem_axes + tile_axes + [both.ndim - 1]).reshape(
        mem_count * tile_count, -1
    )
    x_full = both[:, :x_size].reshape(mem_count * tile_count * x_rows, x_cols)
    y_full = both[:, x_size:].reshape(mem_count * tile_count * y_rows, y_cols)
    return x_full, y_full, after


def body(
    source_blocks, send_blocks, recv_slot, recv_weight, recv_count, regional, x_operator, y_operator
):
    tile_count = lax.axis_size("tile")
    member_count, level_count, columns, y_cells = regional.shape
    capacity = send_blocks.shape[2]
    block_cells = source_blocks.shape[3]
    block_side = math.isqrt(block_cells)
    picked = send_blocks[0].reshape(-1)
    packed = jnp.take(source_blocks, picked, axis=0).reshape(
        tile_count, capacity, member_count, level_count, block_cells
    )
    arrived = lax.all_to_all(packed, "tile", split_axis=0, concat_axis=0, tiled=True)
    x_full, y_full, arrived = gather_operators(x_operator, y_operator, arrived)
    slot_count = columns // block_side * (y_cells // block_side)
    live_mask = lax.broadcasted_iota(jnp.int32, (tile_count, capacity), 1) < recv_count[0][:, None]
    weights = jnp.where(live_mask, recv_weight[0], 0.0).reshape(-1)
    slot_match = recv_slot[0].reshape(-1)[None, :] == lax.broadcasted_iota(
        jnp.int32, (slot_count, tile_count * capacity), 0
    )
    remap_weights = jnp.where(slot_match, weights[None, :], 0.0).astype(jnp.bfloat16)
    remapped = jnp.dot(
        remap_weights,
        arrived.reshape(tile_count * capacity, -1),
        preferred_element_type=jnp.float32,
    )
    remapped = remapped.reshape(
        columns // block_side,
        y_cells // block_side,
        member_count,
        level_count,
        block_side,
        block_side,
    )
    remapped = remapped.transpose(2, 3, 0, 4, 1, 5).reshape(
        member_count, level_count, columns, y_cells
    )
    difference = (remapped - regional.astype(jnp.float32)).astype(jnp.bfloat16)
    x_lines = lax.all_to_all(difference, "tile", split_axis=3, concat_axis=2, tiled=True)
    after_first = jnp.einsum(
        "ax,mlxy->mlay",
        x_full,
        x_lines,
        preferred_element_type=jnp.float32,
    ).astype(jnp.bfloat16)
    tile_back = lax.all_to_all(after_first, "tile", split_axis=2, concat_axis=3, tiled=True)
    after_second = jnp.einsum(
        "by,mlxy->mlxb",
        y_full,
        tile_back,
        preferred_element_type=jnp.float32,
    )
    return (regional.astype(jnp.float32) + after_second).astype(jnp.bfloat16)


def solution(mesh):
    placed = (
        P("tile", "mem", None, None),
        P("tile", None, None),
        P("tile", None, None),
        P("tile", None, None),
        P("tile", None),
        P("mem", None, "tile", None),
        P(("mem", "tile"), None),
        P(("mem", "tile"), None),
    )
    return jax.shard_map(
        body, mesh=mesh, in_specs=placed, out_specs=P("mem", None, "tile", None), check_vma=False
    )
```

```python
import math

import jax
import jax.numpy as jnp
from jax import lax
from jax.sharding import PartitionSpec as P


def doubling_gather(data, axis_name, bits):
    count = lax.axis_size(axis_name)
    index = lax.axis_index(axis_name)
    for bit in bits:
        received = lax.ppermute(data, axis_name, [(j, j ^ bit) for j in range(count)])
        high = (index // bit) % 2 == 1
        data = jnp.stack([jnp.where(high, received, data), jnp.where(high, data, received)])
    return data


def bit_order(count, bits):
    stacked = list(reversed(bits))
    return [stacked.index(bit) for bit in sorted(bits, reverse=True)]


def gather_operators(x_operator, y_operator, after):
    mem_count = lax.axis_size("mem")
    tile_count = lax.axis_size("tile")
    x_rows, x_cols = x_operator.shape
    y_rows, y_cols = y_operator.shape
    x_size = x_rows * x_cols
    both = jnp.concatenate([x_operator.reshape(-1), y_operator.reshape(-1)])
    mem_bits = [1 << k for k in range(mem_count.bit_length() - 1)]
    tile_bits = [1 << k for k in range(1, tile_count.bit_length() - 1)] + [1]
    both = doubling_gather(both, "mem", mem_bits)
    both, after = lax.optimization_barrier((both, after))
    both = doubling_gather(both, "tile", tile_bits)
    tile_axes = bit_order(tile_count, tile_bits)
    mem_axes = [len(tile_bits) + k for k in bit_order(mem_count, mem_bits)]
    both = both.transpose(mem_axes + tile_axes + [both.ndim - 1]).reshape(
        mem_count * tile_count, -1
    )
    x_full = both[:, :x_size].reshape(mem_count * tile_count * x_rows, x_cols)
    y_full = both[:, x_size:].reshape(mem_count * tile_count * y_rows, y_cols)
    return x_full, y_full, after


def body(
    source_blocks, send_blocks, recv_slot, recv_weight, recv_count, regional, x_operator, y_operator
):
    tile_count = lax.axis_size("tile")
    member_count, level_count, columns, y_cells = regional.shape
    capacity = send_blocks.shape[2]
    block_cells = source_blocks.shape[3]
    block_side = math.isqrt(block_cells)
    picked = send_blocks[0].reshape(-1)
    packed = jnp.take(source_blocks, picked, axis=0).reshape(
        tile_count, capacity, member_count, level_count, block_cells
    )
    arrived = lax.all_to_all(packed, "tile", split_axis=0, concat_axis=0, tiled=True)
    x_full, y_full, arrived = gather_operators(x_operator, y_operator, arrived)
    sx_count = columns // block_side
    y_blocks = y_cells // block_side
    j_count = y_blocks // tile_count
    y_chunk = y_cells // tile_count
    live_mask = lax.broadcasted_iota(jnp.int32, (tile_count, capacity), 1) < recv_count[0][:, None]
    weights = jnp.where(live_mask, recv_weight[0], 0.0).reshape(-1)
    row = lax.broadcasted_iota(jnp.int32, (tile_count, sx_count, j_count), 0) * j_count
    row = row + lax.broadcasted_iota(jnp.int32, (tile_count, sx_count, j_count), 1) * y_blocks
    row = row + lax.broadcasted_iota(jnp.int32, (tile_count, sx_count, j_count), 2)
    slot_match = recv_slot[0].reshape(-1)[None, :] == row.reshape(-1)[:, None]
    remap_weights = jnp.where(slot_match, weights[None, :], 0.0).astype(jnp.bfloat16)
    remapped = jnp.dot(
        remap_weights,
        arrived.reshape(tile_count * capacity, -1),
        preferred_element_type=jnp.float32,
    )
    remapped = remapped.reshape(
        tile_count, sx_count, j_count, member_count, level_count, block_side, block_side
    ).transpose(0, 1, 5, 3, 4, 2, 6)
    local_regional = regional.reshape(
        member_count, level_count, sx_count, block_side, tile_count, j_count, block_side
    ).transpose(4, 2, 3, 0, 1, 5, 6)
    difference = (remapped - local_regional.astype(jnp.float32)).astype(jnp.bfloat16)
    x_lines = lax.all_to_all(
        difference.reshape(tile_count, columns, -1), "tile", split_axis=0, concat_axis=0, tiled=True
    )
    after_first = jnp.dot(
        x_full, x_lines.reshape(tile_count * columns, -1), preferred_element_type=jnp.float32
    ).astype(jnp.bfloat16)
    after_first = after_first.reshape(
        tile_count * columns, member_count, level_count, y_chunk
    ).transpose(1, 2, 0, 3)
    tile_back = lax.all_to_all(after_first, "tile", split_axis=2, concat_axis=3, tiled=True)
    after_second = jnp.einsum(
        "by,mlxy->mlxb",
        y_full,
        tile_back,
        preferred_element_type=jnp.float32,
    )
    return (regional.astype(jnp.float32) + after_second).astype(jnp.bfloat16)


def solution(mesh):
    placed = (
        P("tile", "mem", None, None),
        P("tile", None, None),
        P("tile", None, None),
        P("tile", None, None),
        P("tile", None),
        P("mem", None, "tile", None),
        P(("mem", "tile"), None),
        P(("mem", "tile"), None),
    )
    return jax.shard_map(
        body, mesh=mesh, in_specs=placed, out_specs=P("mem", None, "tile", None), check_vma=False
    )
```

```python
import math

import jax
import jax.numpy as jnp
from jax import lax
from jax.sharding import PartitionSpec as P


def doubling_gather(data, axis_name, bits):
    count = lax.axis_size(axis_name)
    for bit in bits:
        received = lax.ppermute(data, axis_name, [(j, j ^ bit) for j in range(count)])
        data = jnp.stack([data, received])
    return data


def stacked_position(offset, bits):
    position = jnp.zeros_like(offset)
    for bit in reversed(bits):
        position = position * 2 + (offset // bit) % 2
    return position


def gather_operators(x_operator, y_operator, after):
    mem_count = lax.axis_size("mem")
    tile_count = lax.axis_size("tile")
    x_rows, x_cols = x_operator.shape
    y_rows, y_cols = y_operator.shape
    x_size = x_rows * x_cols
    both = jnp.concatenate([x_operator.reshape(-1), y_operator.reshape(-1)])
    mem_bits = [1 << k for k in range(mem_count.bit_length() - 1)]
    tile_bits = [1 << k for k in range(1, tile_count.bit_length() - 1)] + [1]
    both = doubling_gather(both, "mem", mem_bits)
    both, after = lax.optimization_barrier((both, after))
    both = doubling_gather(both, "tile", tile_bits).reshape(mem_count * tile_count, -1)
    mem_of = lax.broadcasted_iota(jnp.int32, (mem_count, tile_count), 0)
    tile_of = lax.broadcasted_iota(jnp.int32, (mem_count, tile_count), 1)
    position = stacked_position(tile_of ^ lax.axis_index("tile"), tile_bits) * mem_count
    position = position + stacked_position(mem_of ^ lax.axis_index("mem"), mem_bits)
    position = position.reshape(-1)
    x_full = jnp.take(both[:, :x_size], position, axis=0, mode="clip")
    y_full = jnp.take(both[:, x_size:], position, axis=0, mode="clip")
    x_full = x_full.reshape(mem_count * tile_count * x_rows, x_cols)
    y_full = y_full.reshape(mem_count * tile_count * y_rows, y_cols)
    return x_full, y_full, after


def body(
    source_blocks, send_blocks, recv_slot, recv_weight, recv_count, regional, x_operator, y_operator
):
    tile_count = lax.axis_size("tile")
    member_count, level_count, columns, y_cells = regional.shape
    capacity = send_blocks.shape[2]
    block_cells = source_blocks.shape[3]
    block_side = math.isqrt(block_cells)
    picked = send_blocks[0].reshape(-1)
    packed = jnp.take(source_blocks, picked, axis=0, mode="clip").reshape(
        tile_count, capacity, member_count, level_count, block_cells
    )
    arrived = lax.all_to_all(packed, "tile", split_axis=0, concat_axis=0, tiled=True)
    x_full, y_full, arrived = gather_operators(x_operator, y_operator, arrived)
    slot_count = columns // block_side * (y_cells // block_side)
    live_mask = lax.broadcasted_iota(jnp.int32, (tile_count, capacity), 1) < recv_count[0][:, None]
    weights = jnp.where(live_mask, recv_weight[0], 0.0).reshape(-1)
    slot_match = recv_slot[0].reshape(-1)[None, :] == lax.broadcasted_iota(
        jnp.int32, (slot_count, tile_count * capacity), 0
    )
    remap_weights = jnp.where(slot_match, weights[None, :], 0.0).astype(jnp.bfloat16)
    remapped = jnp.dot(
        remap_weights,
        arrived.reshape(tile_count * capacity, -1),
        preferred_element_type=jnp.float32,
    )
    remapped = remapped.reshape(
        columns // block_side,
        y_cells // block_side,
        member_count,
        level_count,
        block_side,
        block_side,
    )
    remapped = remapped.transpose(2, 3, 0, 4, 1, 5).reshape(
        member_count, level_count, columns, y_cells
    )
    difference = (remapped - regional.astype(jnp.float32)).astype(jnp.bfloat16)
    x_lines = lax.all_to_all(difference, "tile", split_axis=3, concat_axis=2, tiled=True)
    after_first = jnp.einsum(
        "ax,mlxy->mlay",
        x_full,
        x_lines,
        preferred_element_type=jnp.float32,
    ).astype(jnp.bfloat16)
    tile_back = lax.all_to_all(after_first, "tile", split_axis=2, concat_axis=3, tiled=True)
    after_second = jnp.einsum(
        "by,mlxy->mlxb",
        y_full,
        tile_back,
        preferred_element_type=jnp.float32,
    )
    return (regional.astype(jnp.float32) + after_second).astype(jnp.bfloat16)


def solution(mesh):
    placed = (
        P("tile", "mem", None, None),
        P("tile", None, None),
        P("tile", None, None),
        P("tile", None, None),
        P("tile", None),
        P("mem", None, "tile", None),
        P(("mem", "tile"), None),
        P(("mem", "tile"), None),
    )
    return jax.shard_map(
        body, mesh=mesh, in_specs=placed, out_specs=P("mem", None, "tile", None), check_vma=False
    )
```

```python
import math

import jax
import jax.numpy as jnp
from jax import lax
from jax.sharding import PartitionSpec as P


def doubling_gather(data, axis_name, bits):
    count = lax.axis_size(axis_name)
    for bit in bits:
        received = lax.ppermute(data, axis_name, [(j, j ^ bit) for j in range(count)])
        data = jnp.stack([data, received])
    return data


def stacked_position(offset, bits):
    position = jnp.zeros_like(offset)
    for bit in reversed(bits):
        position = position * 2 + (offset // bit) % 2
    return position


def gather_operators(x_operator, y_operator, after):
    mem_count = lax.axis_size("mem")
    tile_count = lax.axis_size("tile")
    x_rows, x_cols = x_operator.shape
    y_rows, y_cols = y_operator.shape
    x_size = x_rows * x_cols
    both = jnp.concatenate([x_operator.reshape(-1), y_operator.reshape(-1)])
    tile_bits = [1 << k for k in range(1, tile_count.bit_length() - 1)] + [1]
    copies = jnp.broadcast_to(both[None], (mem_count,) + both.shape)
    both = lax.all_to_all(copies, "mem", split_axis=0, concat_axis=0, tiled=True)
    both, after = lax.optimization_barrier((both, after))
    both = doubling_gather(both, "tile", tile_bits).reshape(mem_count * tile_count, -1)
    mem_of = lax.broadcasted_iota(jnp.int32, (mem_count, tile_count), 0)
    tile_of = lax.broadcasted_iota(jnp.int32, (mem_count, tile_count), 1)
    position = stacked_position(tile_of ^ lax.axis_index("tile"), tile_bits) * mem_count
    position = position + mem_of
    position = position.reshape(-1)
    x_full = jnp.take(both[:, :x_size], position, axis=0, mode="clip")
    y_full = jnp.take(both[:, x_size:], position, axis=0, mode="clip")
    x_full = x_full.reshape(mem_count * tile_count * x_rows, x_cols)
    y_full = y_full.reshape(mem_count * tile_count * y_rows, y_cols)
    return x_full, y_full, after


def body(
    source_blocks, send_blocks, recv_slot, recv_weight, recv_count, regional, x_operator, y_operator
):
    tile_count = lax.axis_size("tile")
    member_count, level_count, columns, y_cells = regional.shape
    capacity = send_blocks.shape[2]
    block_cells = source_blocks.shape[3]
    block_side = math.isqrt(block_cells)
    picked = send_blocks[0].reshape(-1)
    packed = jnp.take(source_blocks, picked, axis=0, mode="clip").reshape(
        tile_count, capacity, member_count, level_count, block_cells
    )
    arrived = lax.all_to_all(packed, "tile", split_axis=0, concat_axis=0, tiled=True)
    x_full, y_full, arrived = gather_operators(x_operator, y_operator, arrived)
    slot_count = columns // block_side * (y_cells // block_side)
    live_mask = lax.broadcasted_iota(jnp.int32, (tile_count, capacity), 1) < recv_count[0][:, None]
    weights = jnp.where(live_mask, recv_weight[0], 0.0).reshape(-1)
    slot_match = recv_slot[0].reshape(-1)[None, :] == lax.broadcasted_iota(
        jnp.int32, (slot_count, tile_count * capacity), 0
    )
    remap_weights = jnp.where(slot_match, weights[None, :], 0.0).astype(jnp.bfloat16)
    remapped = jnp.dot(
        remap_weights,
        arrived.reshape(tile_count * capacity, -1),
        preferred_element_type=jnp.float32,
    )
    remapped = remapped.reshape(
        columns // block_side,
        y_cells // block_side,
        member_count,
        level_count,
        block_side,
        block_side,
    )
    remapped = remapped.transpose(2, 3, 0, 4, 1, 5).reshape(
        member_count, level_count, columns, y_cells
    )
    difference = (remapped - regional.astype(jnp.float32)).astype(jnp.bfloat16)
    x_lines = lax.all_to_all(difference, "tile", split_axis=3, concat_axis=2, tiled=True)
    after_first = jnp.einsum(
        "ax,mlxy->mlay",
        x_full,
        x_lines,
        preferred_element_type=jnp.float32,
    ).astype(jnp.bfloat16)
    tile_back = lax.all_to_all(after_first, "tile", split_axis=2, concat_axis=3, tiled=True)
    after_second = jnp.einsum(
        "by,mlxy->mlxb",
        y_full,
        tile_back,
        preferred_element_type=jnp.float32,
    )
    return (regional.astype(jnp.float32) + after_second).astype(jnp.bfloat16)


def solution(mesh):
    placed = (
        P("tile", "mem", None, None),
        P("tile", None, None),
        P("tile", None, None),
        P("tile", None, None),
        P("tile", None),
        P("mem", None, "tile", None),
        P(("mem", "tile"), None),
        P(("mem", "tile"), None),
    )
    return jax.shard_map(
        body, mesh=mesh, in_specs=placed, out_specs=P("mem", None, "tile", None), check_vma=False
    )
```

```python
import math

import jax
import jax.numpy as jnp
from jax import lax
from jax.sharding import PartitionSpec as P


def doubling_gather(data, axis_name, bits):
    count = lax.axis_size(axis_name)
    for bit in bits:
        received = lax.ppermute(data, axis_name, [(j, j ^ bit) for j in range(count)])
        data = jnp.stack([data, received])
    return data


def stacked_position(offset, bits):
    position = jnp.zeros_like(offset)
    for bit in reversed(bits):
        position = position * 2 + (offset // bit) % 2
    return position


def gather_operators(x_operator, y_operator, after):
    mem_count = lax.axis_size("mem")
    tile_count = lax.axis_size("tile")
    x_rows, x_cols = x_operator.shape
    y_rows, y_cols = y_operator.shape
    x_size = x_rows * x_cols
    both = jnp.concatenate([x_operator.reshape(-1), y_operator.reshape(-1)])
    mem_bits = [1 << k for k in range(mem_count.bit_length() - 1)]
    tile_bits = [1 << k for k in range(1, tile_count.bit_length() - 1)] + [1]
    both = doubling_gather(both, "mem", mem_bits)
    both, after = lax.optimization_barrier((both, after))
    both = doubling_gather(both, "tile", tile_bits).reshape(mem_count * tile_count, -1)
    mem_of = lax.broadcasted_iota(jnp.int32, (mem_count, tile_count), 0)
    tile_of = lax.broadcasted_iota(jnp.int32, (mem_count, tile_count), 1)
    position = stacked_position(tile_of ^ lax.axis_index("tile"), tile_bits) * mem_count
    position = position + stacked_position(mem_of ^ lax.axis_index("mem"), mem_bits)
    position = position.reshape(-1)
    x_full = jnp.take(both[:, :x_size], position, axis=0, mode="clip")
    y_full = jnp.take(both[:, x_size:], position, axis=0, mode="clip")
    x_full = x_full.reshape(mem_count * tile_count * x_rows, x_cols)
    y_full = y_full.reshape(mem_count * tile_count * y_rows, y_cols)
    return x_full, y_full, after


def body(
    source_blocks, send_blocks, recv_slot, recv_weight, recv_count, regional, x_operator, y_operator
):
    tile_count = lax.axis_size("tile")
    member_count, level_count, columns, y_cells = regional.shape
    capacity = send_blocks.shape[2]
    block_cells = source_blocks.shape[3]
    block_side = math.isqrt(block_cells)
    picked = send_blocks[0].reshape(-1)
    packed = jnp.take(source_blocks, picked, axis=0, mode="clip").reshape(
        tile_count, capacity, member_count, level_count, block_cells
    )
    arrived = lax.all_to_all(packed, "tile", split_axis=0, concat_axis=0, tiled=True)
    x_full, y_full, arrived = gather_operators(x_operator, y_operator, arrived)
    sx_count = columns // block_side
    y_blocks = y_cells // block_side
    j_count = y_blocks // tile_count
    y_chunk = y_cells // tile_count
    live_mask = lax.broadcasted_iota(jnp.int32, (tile_count, capacity), 1) < recv_count[0][:, None]
    weights = jnp.where(live_mask, recv_weight[0], 0.0).reshape(-1)
    row = lax.broadcasted_iota(jnp.int32, (tile_count, sx_count, j_count), 0) * j_count
    row = row + lax.broadcasted_iota(jnp.int32, (tile_count, sx_count, j_count), 1) * y_blocks
    row = row + lax.broadcasted_iota(jnp.int32, (tile_count, sx_count, j_count), 2)
    slot_match = recv_slot[0].reshape(-1)[None, :] == row.reshape(-1)[:, None]
    remap_weights = jnp.where(slot_match, weights[None, :], 0.0).astype(jnp.bfloat16)
    remapped = jnp.dot(
        remap_weights,
        arrived.reshape(tile_count * capacity, -1),
        preferred_element_type=jnp.float32,
    )
    local_regional = regional.reshape(
        member_count, level_count, sx_count, block_side, tile_count, j_count, block_side
    ).transpose(4, 2, 5, 0, 1, 3, 6).reshape(remapped.shape)
    difference = (remapped - local_regional.astype(jnp.float32)).astype(jnp.bfloat16)
    lines = lax.all_to_all(
        difference.reshape(tile_count, sx_count * j_count, -1),
        "tile",
        split_axis=0,
        concat_axis=0,
        tiled=True,
    )
    x_lines = lines.reshape(
        tile_count, sx_count, j_count, member_count, level_count, block_side, block_side
    ).transpose(0, 1, 5, 3, 4, 2, 6).reshape(tile_count * columns, -1)
    after_first = jnp.dot(x_full, x_lines, preferred_element_type=jnp.float32).astype(jnp.bfloat16)
    after_first = after_first.reshape(
        tile_count * columns, member_count, level_count, y_chunk
    ).transpose(1, 2, 0, 3)
    tile_back = lax.all_to_all(after_first, "tile", split_axis=2, concat_axis=3, tiled=True)
    after_second = jnp.einsum(
        "by,mlxy->mlxb",
        y_full,
        tile_back,
        preferred_element_type=jnp.float32,
    )
    return (regional.astype(jnp.float32) + after_second).astype(jnp.bfloat16)


def solution(mesh):
    placed = (
        P("tile", "mem", None, None),
        P("tile", None, None),
        P("tile", None, None),
        P("tile", None, None),
        P("tile", None),
        P("mem", None, "tile", None),
        P(("mem", "tile"), None),
        P(("mem", "tile"), None),
    )
    return jax.shard_map(
        body, mesh=mesh, in_specs=placed, out_specs=P("mem", None, "tile", None), check_vma=False
    )
```

```python
import math

import jax
import jax.numpy as jnp
from jax import lax
from jax.sharding import PartitionSpec as P


def xor_gather(data, axis_name, groups):
    count = lax.axis_size(axis_name)
    for group in groups:
        parts = [data]
        for code in range(1, 1 << len(group)):
            offset = sum(bit for k, bit in enumerate(group) if code >> k & 1)
            parts.append(lax.ppermute(data, axis_name, [(j, j ^ offset) for j in range(count)]))
        data = jnp.stack(parts)
    return data


def stacked_position(offset, groups):
    position = jnp.zeros_like(offset)
    for group in reversed(groups):
        digit = sum(((offset // bit) % 2) << k for k, bit in enumerate(group))
        position = position * (1 << len(group)) + digit
    return position


def bit_groups(bits):
    return [bits[k : k + 2] for k in range(0, len(bits), 2)]


def gather_operators(x_operator, y_operator, after):
    mem_count = lax.axis_size("mem")
    tile_count = lax.axis_size("tile")
    x_rows, x_cols = x_operator.shape
    y_rows, y_cols = y_operator.shape
    x_size = x_rows * x_cols
    both = jnp.concatenate([x_operator.reshape(-1), y_operator.reshape(-1)])
    mem_bits = bit_groups([1 << k for k in range(mem_count.bit_length() - 1)])
    tile_bits = bit_groups([1 << k for k in range(1, tile_count.bit_length() - 1)]) + [[1]]
    both = xor_gather(both, "mem", mem_bits)
    both, after = lax.optimization_barrier((both, after))
    both = xor_gather(both, "tile", tile_bits).reshape(mem_count * tile_count, -1)
    mem_of = lax.broadcasted_iota(jnp.int32, (mem_count, tile_count), 0)
    tile_of = lax.broadcasted_iota(jnp.int32, (mem_count, tile_count), 1)
    position = stacked_position(tile_of ^ lax.axis_index("tile"), tile_bits) * mem_count
    position = position + stacked_position(mem_of ^ lax.axis_index("mem"), mem_bits)
    position = position.reshape(-1)
    x_full = jnp.take(both[:, :x_size], position, axis=0, mode="clip")
    y_full = jnp.take(both[:, x_size:], position, axis=0, mode="clip")
    x_full = x_full.reshape(mem_count * tile_count * x_rows, x_cols)
    y_full = y_full.reshape(mem_count * tile_count * y_rows, y_cols)
    return x_full, y_full, after


def body(
    source_blocks, send_blocks, recv_slot, recv_weight, recv_count, regional, x_operator, y_operator
):
    tile_count = lax.axis_size("tile")
    member_count, level_count, columns, y_cells = regional.shape
    capacity = send_blocks.shape[2]
    block_cells = source_blocks.shape[3]
    block_side = math.isqrt(block_cells)
    picked = send_blocks[0].reshape(-1)
    packed = jnp.take(source_blocks, picked, axis=0, mode="clip").reshape(
        tile_count, capacity, member_count, level_count, block_cells
    )
    arrived = lax.all_to_all(packed, "tile", split_axis=0, concat_axis=0, tiled=True)
    x_full, y_full, arrived = gather_operators(x_operator, y_operator, arrived)
    slot_count = columns // block_side * (y_cells // block_side)
    live_mask = lax.broadcasted_iota(jnp.int32, (tile_count, capacity), 1) < recv_count[0][:, None]
    weights = jnp.where(live_mask, recv_weight[0], 0.0).reshape(-1)
    slot_match = recv_slot[0].reshape(-1)[None, :] == lax.broadcasted_iota(
        jnp.int32, (slot_count, tile_count * capacity), 0
    )
    remap_weights = jnp.where(slot_match, weights[None, :], 0.0).astype(jnp.bfloat16)
    remapped = jnp.dot(
        remap_weights,
        arrived.reshape(tile_count * capacity, -1),
        preferred_element_type=jnp.float32,
    )
    remapped = remapped.reshape(
        columns // block_side,
        y_cells // block_side,
        member_count,
        level_count,
        block_side,
        block_side,
    )
    remapped = remapped.transpose(2, 3, 0, 4, 1, 5).reshape(
        member_count, level_count, columns, y_cells
    )
    difference = (remapped - regional.astype(jnp.float32)).astype(jnp.bfloat16)
    x_lines = lax.all_to_all(difference, "tile", split_axis=3, concat_axis=2, tiled=True)
    after_first = jnp.einsum(
        "ax,mlxy->mlay",
        x_full,
        x_lines,
        preferred_element_type=jnp.float32,
    ).astype(jnp.bfloat16)
    tile_back = lax.all_to_all(after_first, "tile", split_axis=2, concat_axis=3, tiled=True)
    after_second = jnp.einsum(
        "by,mlxy->mlxb",
        y_full,
        tile_back,
        preferred_element_type=jnp.float32,
    )
    return (regional.astype(jnp.float32) + after_second).astype(jnp.bfloat16)


def solution(mesh):
    placed = (
        P("tile", "mem", None, None),
        P("tile", None, None),
        P("tile", None, None),
        P("tile", None, None),
        P("tile", None),
        P("mem", None, "tile", None),
        P(("mem", "tile"), None),
        P(("mem", "tile"), None),
    )
    return jax.shard_map(
        body, mesh=mesh, in_specs=placed, out_specs=P("mem", None, "tile", None), check_vma=False
    )
```

```python
import math

import jax
import jax.numpy as jnp
from jax import lax
from jax.sharding import PartitionSpec as P


def xor_gather(data, axis_name, groups):
    count = lax.axis_size(axis_name)
    for group in groups:
        parts = [data]
        for code in range(1, 1 << len(group)):
            offset = sum(bit for k, bit in enumerate(group) if code >> k & 1)
            parts.append(lax.ppermute(data, axis_name, [(j, j ^ offset) for j in range(count)]))
        data = jnp.stack(parts)
    return data


def stacked_position(offset, groups):
    position = jnp.zeros_like(offset)
    for group in reversed(groups):
        digit = sum(((offset // bit) % 2) << k for k, bit in enumerate(group))
        position = position * (1 << len(group)) + digit
    return position


def bit_groups(bits):
    return [bits[k : k + 2] for k in range(0, len(bits), 2)]


def gather_operators(x_operator, y_operator, after):
    mem_count = lax.axis_size("mem")
    tile_count = lax.axis_size("tile")
    x_rows, x_cols = x_operator.shape
    y_rows, y_cols = y_operator.shape
    x_size = x_rows * x_cols
    both = jnp.concatenate([x_operator.reshape(-1), y_operator.reshape(-1)])
    mem_bits = bit_groups([1 << k for k in range(mem_count.bit_length() - 1)])
    tile_bits = bit_groups([1 << k for k in range(1, tile_count.bit_length() - 1)]) + [[1]]
    both, after = lax.optimization_barrier((both, after))
    both = xor_gather(both, "mem", mem_bits)
    both = xor_gather(both, "tile", tile_bits).reshape(mem_count * tile_count, -1)
    mem_of = lax.broadcasted_iota(jnp.int32, (mem_count, tile_count), 0)
    tile_of = lax.broadcasted_iota(jnp.int32, (mem_count, tile_count), 1)
    position = stacked_position(tile_of ^ lax.axis_index("tile"), tile_bits) * mem_count
    position = position + stacked_position(mem_of ^ lax.axis_index("mem"), mem_bits)
    position = position.reshape(-1)
    x_full = jnp.take(both[:, :x_size], position, axis=0, mode="clip")
    y_full = jnp.take(both[:, x_size:], position, axis=0, mode="clip")
    x_full = x_full.reshape(mem_count * tile_count * x_rows, x_cols)
    y_full = y_full.reshape(mem_count * tile_count * y_rows, y_cols)
    return x_full, y_full, after


def body(
    source_blocks, send_blocks, recv_slot, recv_weight, recv_count, regional, x_operator, y_operator
):
    tile_count = lax.axis_size("tile")
    member_count, level_count, columns, y_cells = regional.shape
    capacity = send_blocks.shape[2]
    block_cells = source_blocks.shape[3]
    block_side = math.isqrt(block_cells)
    picked = send_blocks[0].reshape(-1)
    packed = jnp.take(source_blocks, picked, axis=0, mode="clip").reshape(
        tile_count, capacity, member_count, level_count, block_cells
    )
    x_full, y_full, packed = gather_operators(x_operator, y_operator, packed)
    arrived = lax.all_to_all(packed, "tile", split_axis=0, concat_axis=0, tiled=True)
    slot_count = columns // block_side * (y_cells // block_side)
    live_mask = lax.broadcasted_iota(jnp.int32, (tile_count, capacity), 1) < recv_count[0][:, None]
    weights = jnp.where(live_mask, recv_weight[0], 0.0).reshape(-1)
    slot_match = recv_slot[0].reshape(-1)[None, :] == lax.broadcasted_iota(
        jnp.int32, (slot_count, tile_count * capacity), 0
    )
    remap_weights = jnp.where(slot_match, weights[None, :], 0.0).astype(jnp.bfloat16)
    remapped = jnp.dot(
        remap_weights,
        arrived.reshape(tile_count * capacity, -1),
        preferred_element_type=jnp.float32,
    )
    remapped = remapped.reshape(
        columns // block_side,
        y_cells // block_side,
        member_count,
        level_count,
        block_side,
        block_side,
    )
    remapped = remapped.transpose(2, 3, 0, 4, 1, 5).reshape(
        member_count, level_count, columns, y_cells
    )
    difference = (remapped - regional.astype(jnp.float32)).astype(jnp.bfloat16)
    x_lines = lax.all_to_all(difference, "tile", split_axis=3, concat_axis=2, tiled=True)
    after_first = jnp.einsum(
        "ax,mlxy->mlay",
        x_full,
        x_lines,
        preferred_element_type=jnp.float32,
    ).astype(jnp.bfloat16)
    tile_back = lax.all_to_all(after_first, "tile", split_axis=2, concat_axis=3, tiled=True)
    after_second = jnp.einsum(
        "by,mlxy->mlxb",
        y_full,
        tile_back,
        preferred_element_type=jnp.float32,
    )
    return (regional.astype(jnp.float32) + after_second).astype(jnp.bfloat16)


def solution(mesh):
    placed = (
        P("tile", "mem", None, None),
        P("tile", None, None),
        P("tile", None, None),
        P("tile", None, None),
        P("tile", None),
        P("mem", None, "tile", None),
        P(("mem", "tile"), None),
        P(("mem", "tile"), None),
    )
    return jax.shard_map(
        body, mesh=mesh, in_specs=placed, out_specs=P("mem", None, "tile", None), check_vma=False
    )
```

```python
import math

import jax
import jax.numpy as jnp
from jax import lax
from jax.sharding import PartitionSpec as P


def xor_gather(data, axis_name, groups):
    count = lax.axis_size(axis_name)
    for group in groups:
        parts = [data]
        for code in range(1, 1 << len(group)):
            offset = sum(bit for k, bit in enumerate(group) if code >> k & 1)
            parts.append(lax.ppermute(data, axis_name, [(j, j ^ offset) for j in range(count)]))
        data = jnp.stack(parts)
    return data


def stacked_position(offset, groups):
    position = jnp.zeros_like(offset)
    for group in reversed(groups):
        digit = sum(((offset // bit) % 2) << k for k, bit in enumerate(group))
        position = position * (1 << len(group)) + digit
    return position


def bit_groups(bits):
    return [bits[k : k + 2] for k in range(0, len(bits), 2)]


def gather_operators(x_operator, y_operator, after):
    mem_count = lax.axis_size("mem")
    tile_count = lax.axis_size("tile")
    x_rows, x_cols = x_operator.shape
    y_rows, y_cols = y_operator.shape
    width = max(x_cols, y_cols)
    both = jnp.concatenate(
        [
            jnp.pad(x_operator, ((0, 0), (0, width - x_cols))),
            jnp.pad(y_operator, ((0, 0), (0, width - y_cols))),
        ]
    )
    mem_bits = bit_groups([1 << k for k in range(mem_count.bit_length() - 1)])
    tile_bits = bit_groups([1 << k for k in range(1, tile_count.bit_length() - 1)]) + [[1]]
    both = xor_gather(both, "mem", mem_bits)
    both, after = lax.optimization_barrier((both, after))
    both = xor_gather(both, "tile", tile_bits).reshape(mem_count * tile_count, x_rows + y_rows, width)
    mem_of = lax.broadcasted_iota(jnp.int32, (mem_count, tile_count), 0)
    tile_of = lax.broadcasted_iota(jnp.int32, (mem_count, tile_count), 1)
    position = stacked_position(tile_of ^ lax.axis_index("tile"), tile_bits) * mem_count
    position = position + stacked_position(mem_of ^ lax.axis_index("mem"), mem_bits)
    position = position.reshape(-1)
    x_full = jnp.take(both[:, :x_rows, :x_cols], position, axis=0, mode="clip")
    y_full = jnp.take(both[:, x_rows:, :y_cols], position, axis=0, mode="clip")
    x_full = x_full.reshape(mem_count * tile_count * x_rows, x_cols)
    y_full = y_full.reshape(mem_count * tile_count * y_rows, y_cols)
    return x_full, y_full, after


def body(
    source_blocks, send_blocks, recv_slot, recv_weight, recv_count, regional, x_operator, y_operator
):
    tile_count = lax.axis_size("tile")
    member_count, level_count, columns, y_cells = regional.shape
    capacity = send_blocks.shape[2]
    block_cells = source_blocks.shape[3]
    block_side = math.isqrt(block_cells)
    picked = send_blocks[0].reshape(-1)
    held = source_blocks.shape[0]
    one_hot = (picked[:, None] == lax.broadcasted_iota(jnp.int32, (1, held), 1)).astype(
        source_blocks.dtype
    )
    packed = jnp.dot(
        one_hot, source_blocks.reshape(held, -1), preferred_element_type=jnp.float32
    ).astype(source_blocks.dtype)
    packed = packed.reshape(tile_count, capacity, member_count, level_count, block_cells)
    arrived = lax.all_to_all(packed, "tile", split_axis=0, concat_axis=0, tiled=True)
    x_full, y_full, arrived = gather_operators(x_operator, y_operator, arrived)
    slot_count = columns // block_side * (y_cells // block_side)
    live_mask = lax.broadcasted_iota(jnp.int32, (tile_count, capacity), 1) < recv_count[0][:, None]
    weights = jnp.where(live_mask, recv_weight[0], 0.0).reshape(-1)
    slot_match = recv_slot[0].reshape(-1)[None, :] == lax.broadcasted_iota(
        jnp.int32, (slot_count, tile_count * capacity), 0
    )
    remap_weights = jnp.where(slot_match, weights[None, :], 0.0).astype(jnp.bfloat16)
    remapped = jnp.dot(
        remap_weights,
        arrived.reshape(tile_count * capacity, -1),
        preferred_element_type=jnp.float32,
    )
    remapped = remapped.reshape(
        columns // block_side,
        y_cells // block_side,
        member_count,
        level_count,
        block_side,
        block_side,
    )
    remapped = remapped.transpose(2, 3, 0, 4, 1, 5).reshape(
        member_count, level_count, columns, y_cells
    )
    difference = (remapped - regional.astype(jnp.float32)).astype(jnp.bfloat16)
    x_lines = lax.all_to_all(difference, "tile", split_axis=3, concat_axis=2, tiled=True)
    after_first = jnp.einsum(
        "ax,mlxy->mlay",
        x_full,
        x_lines,
        preferred_element_type=jnp.float32,
    ).astype(jnp.bfloat16)
    tile_back = lax.all_to_all(after_first, "tile", split_axis=2, concat_axis=3, tiled=True)
    after_second = jnp.einsum(
        "by,mlxy->mlxb",
        y_full,
        tile_back,
        preferred_element_type=jnp.float32,
    )
    return (regional.astype(jnp.float32) + after_second).astype(jnp.bfloat16)


def solution(mesh):
    placed = (
        P("tile", "mem", None, None),
        P("tile", None, None),
        P("tile", None, None),
        P("tile", None, None),
        P("tile", None),
        P("mem", None, "tile", None),
        P(("mem", "tile"), None),
        P(("mem", "tile"), None),
    )
    return jax.shard_map(
        body, mesh=mesh, in_specs=placed, out_specs=P("mem", None, "tile", None), check_vma=False
    )
```

```python
import math

import jax
import jax.numpy as jnp
from jax import lax
from jax.sharding import PartitionSpec as P


def xor_gather(data, axis_name, groups):
    count = lax.axis_size(axis_name)
    for group in groups:
        parts = [data]
        for code in range(1, 1 << len(group)):
            offset = sum(bit for k, bit in enumerate(group) if code >> k & 1)
            parts.append(lax.ppermute(data, axis_name, [(j, j ^ offset) for j in range(count)]))
        data = jnp.stack(parts)
    return data


def stacked_position(offset, groups):
    position = jnp.zeros_like(offset)
    for group in reversed(groups):
        digit = sum(((offset // bit) % 2) << k for k, bit in enumerate(group))
        position = position * (1 << len(group)) + digit
    return position


def bit_groups(bits):
    return [bits[k : k + 2] for k in range(0, len(bits), 2)]


def gather_operators(x_operator, y_operator, after):
    mem_count = lax.axis_size("mem")
    tile_count = lax.axis_size("tile")
    x_rows, x_cols = x_operator.shape
    y_rows, y_cols = y_operator.shape
    width = max(x_cols, y_cols)
    both = jnp.concatenate(
        [
            jnp.pad(x_operator, ((0, 0), (0, width - x_cols))),
            jnp.pad(y_operator, ((0, 0), (0, width - y_cols))),
        ]
    )
    mem_bits = bit_groups([1 << k for k in range(mem_count.bit_length() - 1)])
    tile_bits = bit_groups([1 << k for k in range(1, tile_count.bit_length() - 1)]) + [[1]]
    both = xor_gather(both, "mem", mem_bits)
    both, after = lax.optimization_barrier((both, after))
    both = xor_gather(both, "tile", tile_bits).reshape(mem_count * tile_count, x_rows + y_rows, width)
    mem_of = lax.broadcasted_iota(jnp.int32, (mem_count, tile_count), 0)
    tile_of = lax.broadcasted_iota(jnp.int32, (mem_count, tile_count), 1)
    position = stacked_position(tile_of ^ lax.axis_index("tile"), tile_bits) * mem_count
    position = position + stacked_position(mem_of ^ lax.axis_index("mem"), mem_bits)
    position = position.reshape(-1)
    x_full = jnp.take(both[:, :x_rows, :x_cols], position, axis=0, mode="clip")
    y_full = jnp.take(both[:, x_rows:, :y_cols], position, axis=0, mode="clip")
    x_full = x_full.reshape(mem_count * tile_count * x_rows, x_cols)
    y_full = y_full.reshape(mem_count * tile_count * y_rows, y_cols)
    return x_full, y_full, after


def body(
    source_blocks, send_blocks, recv_slot, recv_weight, recv_count, regional, x_operator, y_operator
):
    tile_count = lax.axis_size("tile")
    member_count, level_count, columns, y_cells = regional.shape
    capacity = send_blocks.shape[2]
    block_cells = source_blocks.shape[3]
    block_side = math.isqrt(block_cells)
    picked = send_blocks[0].reshape(-1)
    held = source_blocks.shape[0]
    one_hot = (picked[:, None] == lax.broadcasted_iota(jnp.int32, (1, held), 1)).astype(
        source_blocks.dtype
    )
    packed = jnp.dot(
        one_hot, source_blocks.reshape(held, -1), preferred_element_type=jnp.float32
    ).astype(source_blocks.dtype)
    packed = packed.reshape(tile_count, capacity, -1)
    arrived = lax.all_to_all(packed, "tile", split_axis=0, concat_axis=0, tiled=True)
    x_full, y_full, arrived = gather_operators(x_operator, y_operator, arrived)
    slot_count = columns // block_side * (y_cells // block_side)
    live_mask = lax.broadcasted_iota(jnp.int32, (tile_count, capacity), 1) < recv_count[0][:, None]
    weights = jnp.where(live_mask, recv_weight[0], 0.0).reshape(-1)
    slot_match = recv_slot[0].reshape(-1)[None, :] == lax.broadcasted_iota(
        jnp.int32, (slot_count, tile_count * capacity), 0
    )
    remap_weights = jnp.where(slot_match, weights[None, :], 0.0).astype(jnp.bfloat16)
    remapped = jnp.dot(
        remap_weights,
        arrived.reshape(tile_count * capacity, -1),
        preferred_element_type=jnp.float32,
    )
    remapped = remapped.reshape(
        columns // block_side,
        y_cells // block_side,
        member_count,
        level_count,
        block_side,
        block_side,
    )
    remapped = remapped.transpose(2, 3, 0, 4, 1, 5).reshape(
        member_count, level_count, columns, y_cells
    )
    difference = (remapped - regional.astype(jnp.float32)).astype(jnp.bfloat16)
    x_lines = lax.all_to_all(difference, "tile", split_axis=3, concat_axis=2, tiled=True)
    after_first = jnp.einsum(
        "ax,mlxy->mlay",
        x_full,
        x_lines,
        preferred_element_type=jnp.float32,
    ).astype(jnp.bfloat16)
    tile_back = lax.all_to_all(after_first, "tile", split_axis=2, concat_axis=3, tiled=True)
    after_second = jnp.einsum(
        "by,mlxy->mlxb",
        y_full,
        tile_back,
        preferred_element_type=jnp.float32,
    )
    return (regional.astype(jnp.float32) + after_second).astype(jnp.bfloat16)


def solution(mesh):
    placed = (
        P("tile", "mem", None, None),
        P("tile", None, None),
        P("tile", None, None),
        P("tile", None, None),
        P("tile", None),
        P("mem", None, "tile", None),
        P(("mem", "tile"), None),
        P(("mem", "tile"), None),
    )
    return jax.shard_map(
        body, mesh=mesh, in_specs=placed, out_specs=P("mem", None, "tile", None), check_vma=False
    )
```

```python
import math

import jax
import jax.numpy as jnp
from jax import lax
from jax.sharding import PartitionSpec as P


def xor_gather(data, axis_name, groups):
    count = lax.axis_size(axis_name)
    for group in groups:
        parts = [data]
        for code in range(1, 1 << len(group)):
            offset = sum(bit for k, bit in enumerate(group) if code >> k & 1)
            parts.append(lax.ppermute(data, axis_name, [(j, j ^ offset) for j in range(count)]))
        data = jnp.stack(parts)
    return data


def stacked_position(offset, groups):
    position = jnp.zeros_like(offset)
    for group in reversed(groups):
        digit = sum(((offset // bit) % 2) << k for k, bit in enumerate(group))
        position = position * (1 << len(group)) + digit
    return position


def bit_groups(bits):
    return [bits[k : k + 2] for k in range(0, len(bits), 2)]


def gather_operators(x_operator, y_operator, after):
    mem_count = lax.axis_size("mem")
    tile_count = lax.axis_size("tile")
    x_rows, x_cols = x_operator.shape
    y_rows, y_cols = y_operator.shape
    width = max(x_cols, y_cols)
    both = jnp.concatenate(
        [
            jnp.pad(x_operator, ((0, 0), (0, width - x_cols))),
            jnp.pad(y_operator, ((0, 0), (0, width - y_cols))),
        ]
    )
    mem_bits = bit_groups([1 << k for k in range(mem_count.bit_length() - 1)])
    tile_bits = bit_groups([1 << k for k in range(1, tile_count.bit_length() - 1)]) + [[1]]
    both = xor_gather(both, "mem", mem_bits)
    both, after = lax.optimization_barrier((both, after))
    both = xor_gather(both, "tile", tile_bits).reshape(mem_count * tile_count, x_rows + y_rows, width)
    mem_of = lax.broadcasted_iota(jnp.int32, (mem_count, tile_count), 0)
    tile_of = lax.broadcasted_iota(jnp.int32, (mem_count, tile_count), 1)
    position = stacked_position(tile_of ^ lax.axis_index("tile"), tile_bits) * mem_count
    position = position + stacked_position(mem_of ^ lax.axis_index("mem"), mem_bits)
    position = position.reshape(-1)
    x_full = jnp.take(both[:, :x_rows, :x_cols], position, axis=0, mode="clip")
    y_full = jnp.take(both[:, x_rows:, :y_cols], position, axis=0, mode="clip")
    x_full = x_full.reshape(mem_count * tile_count * x_rows, x_cols)
    y_full = y_full.reshape(mem_count * tile_count * y_rows, y_cols)
    return x_full, y_full, after


def body(
    source_blocks, send_blocks, recv_slot, recv_weight, recv_count, regional, x_operator, y_operator
):
    tile_count = lax.axis_size("tile")
    member_count, level_count, columns, y_cells = regional.shape
    capacity = send_blocks.shape[2]
    block_cells = source_blocks.shape[3]
    block_side = math.isqrt(block_cells)
    picked = send_blocks[0].reshape(-1)
    held = source_blocks.shape[0]
    one_hot = (picked[:, None] == lax.broadcasted_iota(jnp.int32, (1, held), 1)).astype(
        source_blocks.dtype
    )
    packed = jnp.dot(
        one_hot, source_blocks.reshape(held, -1), preferred_element_type=jnp.float32
    ).astype(source_blocks.dtype)
    packed = packed.reshape(tile_count, capacity, -1)
    arrived = lax.all_to_all(packed, "tile", split_axis=0, concat_axis=0, tiled=True)
    x_full, y_full, arrived = gather_operators(x_operator, y_operator, arrived)
    slot_count = columns // block_side * (y_cells // block_side)
    live_mask = lax.broadcasted_iota(jnp.int32, (tile_count, capacity), 1) < recv_count[0][:, None]
    weights = jnp.where(live_mask, recv_weight[0], 0.0).reshape(-1)
    slot_match = recv_slot[0].reshape(-1)[None, :] == lax.broadcasted_iota(
        jnp.int32, (slot_count, tile_count * capacity), 0
    )
    remap_weights = jnp.where(slot_match, weights[None, :], 0.0).astype(jnp.bfloat16)
    remapped = jnp.dot(
        remap_weights,
        arrived.reshape(tile_count * capacity, -1),
        preferred_element_type=jnp.float32,
    )
    remapped = remapped.reshape(
        columns // block_side,
        y_cells // block_side,
        member_count,
        level_count,
        block_side,
        block_side,
    )
    remapped = remapped.transpose(2, 3, 1, 5, 0, 4).reshape(
        member_count, level_count, y_cells, columns
    )
    y_major = regional.transpose(0, 1, 3, 2)
    difference = (remapped - y_major.astype(jnp.float32)).astype(jnp.bfloat16)
    x_lines = lax.all_to_all(difference, "tile", split_axis=2, concat_axis=3, tiled=True)
    after_first = jnp.einsum(
        "mlyx,ax->mlya", x_lines, x_full, preferred_element_type=jnp.float32
    ).astype(jnp.bfloat16)
    tile_back = lax.all_to_all(after_first, "tile", split_axis=3, concat_axis=2, tiled=True)
    after_second = jnp.einsum(
        "mlyx,by->mlxb", tile_back, y_full, preferred_element_type=jnp.float32
    )
    return (regional.astype(jnp.float32) + after_second).astype(jnp.bfloat16)


def solution(mesh):
    placed = (
        P("tile", "mem", None, None),
        P("tile", None, None),
        P("tile", None, None),
        P("tile", None, None),
        P("tile", None),
        P("mem", None, "tile", None),
        P(("mem", "tile"), None),
        P(("mem", "tile"), None),
    )
    return jax.shard_map(
        body, mesh=mesh, in_specs=placed, out_specs=P("mem", None, "tile", None), check_vma=False
    )
```

```python
import math

import jax
import jax.numpy as jnp
from jax import lax
from jax.sharding import PartitionSpec as P


def xor_gather(data, axis_name, groups):
    count = lax.axis_size(axis_name)
    for group in groups:
        parts = [data]
        for code in range(1, 1 << len(group)):
            offset = sum(bit for k, bit in enumerate(group) if code >> k & 1)
            parts.append(lax.ppermute(data, axis_name, [(j, j ^ offset) for j in range(count)]))
        data = jnp.stack(parts)
    return data


def stacked_position(offset, groups):
    position = jnp.zeros_like(offset)
    for group in reversed(groups):
        digit = sum(((offset // bit) % 2) << k for k, bit in enumerate(group))
        position = position * (1 << len(group)) + digit
    return position


def bit_groups(bits):
    return [bits[k : k + 2] for k in range(0, len(bits), 2)]


def gather_operators(x_operator, y_operator, after):
    mem_count = lax.axis_size("mem")
    tile_count = lax.axis_size("tile")
    x_rows, x_cols = x_operator.shape
    y_rows, y_cols = y_operator.shape
    width = max(x_cols, y_cols)
    both = jnp.concatenate(
        [
            jnp.pad(x_operator, ((0, 0), (0, width - x_cols))),
            jnp.pad(y_operator, ((0, 0), (0, width - y_cols))),
        ]
    )
    mem_bits = bit_groups([1 << k for k in range(mem_count.bit_length() - 1)])
    tile_bits = bit_groups([1 << k for k in range(1, tile_count.bit_length() - 1)]) + [[1]]
    both = xor_gather(both, "mem", mem_bits)
    both = xor_gather(both, "tile", tile_bits[:-1])
    both, after = lax.optimization_barrier((both, after))
    both = xor_gather(both, "tile", tile_bits[-1:]).reshape(
        mem_count * tile_count, x_rows + y_rows, width
    )
    mem_of = lax.broadcasted_iota(jnp.int32, (mem_count, tile_count), 0)
    tile_of = lax.broadcasted_iota(jnp.int32, (mem_count, tile_count), 1)
    position = stacked_position(tile_of ^ lax.axis_index("tile"), tile_bits) * mem_count
    position = position + stacked_position(mem_of ^ lax.axis_index("mem"), mem_bits)
    position = position.reshape(-1)
    x_full = jnp.take(both[:, :x_rows, :x_cols], position, axis=0, mode="clip")
    y_full = jnp.take(both[:, x_rows:, :y_cols], position, axis=0, mode="clip")
    x_full = x_full.reshape(mem_count * tile_count * x_rows, x_cols)
    y_full = y_full.reshape(mem_count * tile_count * y_rows, y_cols)
    return x_full, y_full, after


def body(
    source_blocks, send_blocks, recv_slot, recv_weight, recv_count, regional, x_operator, y_operator
):
    tile_count = lax.axis_size("tile")
    member_count, level_count, columns, y_cells = regional.shape
    capacity = send_blocks.shape[2]
    block_cells = source_blocks.shape[3]
    block_side = math.isqrt(block_cells)
    picked = send_blocks[0].reshape(-1)
    held = source_blocks.shape[0]
    one_hot = (picked[:, None] == lax.broadcasted_iota(jnp.int32, (1, held), 1)).astype(
        source_blocks.dtype
    )
    packed = jnp.dot(
        one_hot, source_blocks.reshape(held, -1), preferred_element_type=jnp.float32
    ).astype(source_blocks.dtype)
    packed = packed.reshape(tile_count, capacity, -1)
    arrived = lax.all_to_all(packed, "tile", split_axis=0, concat_axis=0, tiled=True)
    slot_count = columns // block_side * (y_cells // block_side)
    live_mask = lax.broadcasted_iota(jnp.int32, (tile_count, capacity), 1) < recv_count[0][:, None]
    weights = jnp.where(live_mask, recv_weight[0], 0.0).reshape(-1)
    slot_match = recv_slot[0].reshape(-1)[None, :] == lax.broadcasted_iota(
        jnp.int32, (slot_count, tile_count * capacity), 0
    )
    remap_weights = jnp.where(slot_match, weights[None, :], 0.0).astype(jnp.bfloat16)
    remapped = jnp.dot(
        remap_weights,
        arrived.reshape(tile_count * capacity, -1),
        preferred_element_type=jnp.float32,
    )
    remapped = remapped.reshape(
        columns // block_side,
        y_cells // block_side,
        member_count,
        level_count,
        block_side,
        block_side,
    )
    remapped = remapped.transpose(2, 3, 0, 4, 1, 5).reshape(
        member_count, level_count, columns, y_cells
    )
    difference = (remapped - regional.astype(jnp.float32)).astype(jnp.bfloat16)
    x_full, y_full, difference = gather_operators(x_operator, y_operator, difference)
    x_lines = lax.all_to_all(difference, "tile", split_axis=3, concat_axis=2, tiled=True)
    after_first = jnp.einsum(
        "ax,mlxy->mlay",
        x_full,
        x_lines,
        preferred_element_type=jnp.float32,
    ).astype(jnp.bfloat16)
    tile_back = lax.all_to_all(after_first, "tile", split_axis=2, concat_axis=3, tiled=True)
    after_second = jnp.einsum(
        "by,mlxy->mlxb",
        y_full,
        tile_back,
        preferred_element_type=jnp.float32,
    )
    return (regional.astype(jnp.float32) + after_second).astype(jnp.bfloat16)


def solution(mesh):
    placed = (
        P("tile", "mem", None, None),
        P("tile", None, None),
        P("tile", None, None),
        P("tile", None, None),
        P("tile", None),
        P("mem", None, "tile", None),
        P(("mem", "tile"), None),
        P(("mem", "tile"), None),
    )
    return jax.shard_map(
        body, mesh=mesh, in_specs=placed, out_specs=P("mem", None, "tile", None), check_vma=False
    )
```

```python
import math

import jax
import jax.numpy as jnp
from jax import lax
from jax.sharding import PartitionSpec as P


def xor_gather(data, axis_name, groups):
    count = lax.axis_size(axis_name)
    for group in groups:
        parts = [data]
        for code in range(1, 1 << len(group)):
            offset = sum(bit for k, bit in enumerate(group) if code >> k & 1)
            parts.append(lax.ppermute(data, axis_name, [(j, j ^ offset) for j in range(count)]))
        data = jnp.stack(parts)
    return data


def stacked_position(offset, groups):
    position = jnp.zeros_like(offset)
    for group in reversed(groups):
        digit = sum(((offset // bit) % 2) << k for k, bit in enumerate(group))
        position = position * (1 << len(group)) + digit
    return position


def bit_groups(bits):
    return [bits[k : k + 2] for k in range(0, len(bits), 2)]


def gather_operators(x_operator, y_operator, after):
    mem_count = lax.axis_size("mem")
    tile_count = lax.axis_size("tile")
    x_rows, x_cols = x_operator.shape
    y_rows, y_cols = y_operator.shape
    width = max(x_cols, y_cols)
    both = jnp.concatenate(
        [
            jnp.pad(x_operator, ((0, 0), (0, width - x_cols))),
            jnp.pad(y_operator, ((0, 0), (0, width - y_cols))),
        ]
    )
    mem_bits = bit_groups([1 << k for k in range(mem_count.bit_length() - 1)])
    tile_bits = bit_groups([1 << k for k in range(1, tile_count.bit_length() - 1)]) + [[1]]
    both = xor_gather(both, "mem", mem_bits)
    both, after = lax.optimization_barrier((both, after))
    both = xor_gather(both, "tile", tile_bits).reshape(mem_count * tile_count, x_rows + y_rows, width)
    mem_of = lax.broadcasted_iota(jnp.int32, (mem_count, tile_count), 0)
    tile_of = lax.broadcasted_iota(jnp.int32, (mem_count, tile_count), 1)
    position = stacked_position(tile_of ^ lax.axis_index("tile"), tile_bits) * mem_count
    position = position + stacked_position(mem_of ^ lax.axis_index("mem"), mem_bits)
    position = position.reshape(-1)
    x_full = jnp.take(both[:, :x_rows, :x_cols], position, axis=0, mode="clip")
    y_full = jnp.take(both[:, x_rows:, :y_cols], position, axis=0, mode="clip")
    x_full = x_full.reshape(mem_count * tile_count * x_rows, x_cols)
    y_full = y_full.reshape(mem_count * tile_count * y_rows, y_cols)
    return x_full, y_full, after


def body(
    source_blocks, send_blocks, recv_slot, recv_weight, recv_count, regional, x_operator, y_operator
):
    tile_count = lax.axis_size("tile")
    member_count, level_count, columns, y_cells = regional.shape
    capacity = send_blocks.shape[2]
    block_cells = source_blocks.shape[3]
    block_side = math.isqrt(block_cells)
    picked = send_blocks[0].reshape(-1)
    held = source_blocks.shape[0]
    one_hot = (picked[:, None] == lax.broadcasted_iota(jnp.int32, (1, held), 1)).astype(
        source_blocks.dtype
    )
    packed = jnp.dot(
        one_hot, source_blocks.reshape(held, -1), preferred_element_type=jnp.float32
    ).astype(source_blocks.dtype)
    packed = packed.reshape(tile_count, capacity, -1)
    arrived = lax.all_to_all(packed, "tile", split_axis=0, concat_axis=0, tiled=True)
    x_full, y_full, arrived = gather_operators(x_operator, y_operator, arrived)
    slot_count = columns // block_side * (y_cells // block_side)
    live_mask = lax.broadcasted_iota(jnp.int32, (tile_count, capacity), 1) < recv_count[0][:, None]
    weights = jnp.where(live_mask, recv_weight[0], 0.0).reshape(-1)
    slot_match = recv_slot[0].reshape(-1)[None, :] == lax.broadcasted_iota(
        jnp.int32, (slot_count, tile_count * capacity), 0
    )
    remap_weights = jnp.where(slot_match, weights[None, :], 0.0).astype(jnp.bfloat16)
    remapped = jnp.dot(
        remap_weights,
        arrived.reshape(tile_count * capacity, -1),
        preferred_element_type=jnp.float32,
    )
    remapped = remapped.reshape(
        columns // block_side,
        y_cells // block_side,
        member_count,
        level_count,
        block_side,
        block_side,
    )
    remapped = remapped.transpose(2, 3, 0, 4, 1, 5).reshape(
        member_count, level_count, columns, y_cells
    )
    difference = (remapped - regional.astype(jnp.float32)).astype(jnp.bfloat16)
    x_lines = lax.all_to_all(difference, "tile", split_axis=3, concat_axis=2, tiled=True)
    after_first = jnp.einsum(
        "ax,mlxy->mlay",
        x_full,
        x_lines,
        preferred_element_type=jnp.float32,
    ).astype(jnp.bfloat16)
    y_chunk = y_cells // tile_count
    outgoing = after_first.reshape(
        member_count, level_count, tile_count, columns, y_chunk
    ).transpose(2, 0, 1, 3, 4)
    tile_back = lax.all_to_all(outgoing, "tile", split_axis=0, concat_axis=0, tiled=True)
    after_second = jnp.einsum(
        "tmlxy,bty->mlxb",
        tile_back,
        y_full.reshape(y_cells, tile_count, y_chunk),
        preferred_element_type=jnp.float32,
    )
    return (regional.astype(jnp.float32) + after_second).astype(jnp.bfloat16)


def solution(mesh):
    placed = (
        P("tile", "mem", None, None),
        P("tile", None, None),
        P("tile", None, None),
        P("tile", None, None),
        P("tile", None),
        P("mem", None, "tile", None),
        P(("mem", "tile"), None),
        P(("mem", "tile"), None),
    )
    return jax.shard_map(
        body, mesh=mesh, in_specs=placed, out_specs=P("mem", None, "tile", None), check_vma=False
    )
```

```python
import math

import jax
import jax.numpy as jnp
from jax import lax
from jax.sharding import PartitionSpec as P


def xor_gather(data, axis_name, groups):
    count = lax.axis_size(axis_name)
    for group in groups:
        parts = [data]
        for code in range(1, 1 << len(group)):
            offset = sum(bit for k, bit in enumerate(group) if code >> k & 1)
            parts.append(lax.ppermute(data, axis_name, [(j, j ^ offset) for j in range(count)]))
        data = jnp.stack(parts)
    return data


def stacked_position(offset, groups):
    position = jnp.zeros_like(offset)
    for group in reversed(groups):
        digit = sum(((offset // bit) % 2) << k for k, bit in enumerate(group))
        position = position * (1 << len(group)) + digit
    return position


def bit_groups(bits):
    return [bits[k : k + 2] for k in range(0, len(bits), 2)]


def gather_operators(x_operator, y_operator, after):
    mem_count = lax.axis_size("mem")
    tile_count = lax.axis_size("tile")
    x_rows, x_cols = x_operator.shape
    y_rows, y_cols = y_operator.shape
    width = max(x_cols, y_cols)
    both = jnp.concatenate(
        [
            jnp.pad(x_operator, ((0, 0), (0, width - x_cols))),
            jnp.pad(y_operator, ((0, 0), (0, width - y_cols))),
        ]
    )
    mem_bits = bit_groups([1 << k for k in range(mem_count.bit_length() - 1)])
    tile_bits = bit_groups([1 << k for k in range(1, tile_count.bit_length() - 1)]) + [[1]]
    both = xor_gather(both, "mem", mem_bits)
    both, after = lax.optimization_barrier((both, after))
    both = xor_gather(both, "tile", tile_bits).reshape(mem_count * tile_count, x_rows + y_rows, width)
    mem_of = lax.broadcasted_iota(jnp.int32, (mem_count, tile_count), 0)
    tile_of = lax.broadcasted_iota(jnp.int32, (mem_count, tile_count), 1)
    position = stacked_position(tile_of ^ lax.axis_index("tile"), tile_bits) * mem_count
    position = position + stacked_position(mem_of ^ lax.axis_index("mem"), mem_bits)
    position = position.reshape(-1)
    x_full = jnp.take(both[:, :x_rows, :x_cols], position, axis=0, mode="clip")
    y_full = jnp.take(both[:, x_rows:, :y_cols], position, axis=0, mode="clip")
    x_full = x_full.reshape(mem_count * tile_count * x_rows, x_cols)
    y_full = y_full.reshape(mem_count * tile_count * y_rows, y_cols)
    return x_full, y_full, after


def body(
    source_blocks, send_blocks, recv_slot, recv_weight, recv_count, regional, x_operator, y_operator
):
    tile_count = lax.axis_size("tile")
    member_count, level_count, columns, y_cells = regional.shape
    capacity = send_blocks.shape[2]
    block_cells = source_blocks.shape[3]
    block_side = math.isqrt(block_cells)
    picked = send_blocks[0].reshape(-1)
    held = source_blocks.shape[0]
    one_hot = (picked[:, None] == lax.broadcasted_iota(jnp.int32, (1, held), 1)).astype(
        source_blocks.dtype
    )
    packed = jnp.dot(
        one_hot, source_blocks.reshape(held, -1), preferred_element_type=jnp.float32
    ).astype(source_blocks.dtype)
    packed = packed.reshape(tile_count, capacity, -1)
    arrived = lax.all_to_all(packed, "tile", split_axis=0, concat_axis=0, tiled=True)
    x_full, y_full, arrived = gather_operators(x_operator, y_operator, arrived)
    slot_count = columns // block_side * (y_cells // block_side)
    live_mask = lax.broadcasted_iota(jnp.int32, (tile_count, capacity), 1) < recv_count[0][:, None]
    weights = jnp.where(live_mask, recv_weight[0], 0.0).reshape(-1)
    slot_match = recv_slot[0].reshape(-1)[None, :] == lax.broadcasted_iota(
        jnp.int32, (slot_count, tile_count * capacity), 0
    )
    remap_weights = jnp.where(slot_match, weights[None, :], 0.0).astype(jnp.bfloat16)
    remapped = jnp.dot(
        remap_weights,
        arrived.reshape(tile_count * capacity, -1),
        preferred_element_type=jnp.float32,
    )
    remapped = remapped.reshape(
        columns // block_side,
        y_cells // block_side,
        member_count,
        level_count,
        block_side,
        block_side,
    )
    remapped = remapped.transpose(2, 3, 0, 4, 1, 5).reshape(
        member_count, level_count, columns, y_cells
    )
    difference = (remapped - regional.astype(jnp.float32)).astype(jnp.bfloat16)
    y_chunk = y_cells // tile_count
    sending = difference.reshape(
        member_count, level_count, columns, tile_count, y_chunk
    ).transpose(3, 0, 1, 2, 4)
    x_lines = lax.all_to_all(sending, "tile", split_axis=0, concat_axis=0, tiled=True)
    outgoing = jnp.einsum(
        "dmlxy,tadx->tmlay",
        x_lines,
        x_full.reshape(tile_count, columns, tile_count, columns),
        preferred_element_type=jnp.float32,
    ).astype(jnp.bfloat16)
    tile_back = lax.all_to_all(outgoing, "tile", split_axis=0, concat_axis=0, tiled=True)
    after_second = jnp.einsum(
        "tmlxy,bty->mlxb",
        tile_back,
        y_full.reshape(y_cells, tile_count, y_chunk),
        preferred_element_type=jnp.float32,
    )
    return (regional.astype(jnp.float32) + after_second).astype(jnp.bfloat16)


def solution(mesh):
    placed = (
        P("tile", "mem", None, None),
        P("tile", None, None),
        P("tile", None, None),
        P("tile", None, None),
        P("tile", None),
        P("mem", None, "tile", None),
        P(("mem", "tile"), None),
        P(("mem", "tile"), None),
    )
    return jax.shard_map(
        body, mesh=mesh, in_specs=placed, out_specs=P("mem", None, "tile", None), check_vma=False
    )
```

```python
import math

import jax
import jax.numpy as jnp
from jax import lax
from jax.sharding import PartitionSpec as P


def xor_gather(data, axis_name, groups):
    count = lax.axis_size(axis_name)
    for group in groups:
        parts = [data]
        for code in range(1, 1 << len(group)):
            offset = sum(bit for k, bit in enumerate(group) if code >> k & 1)
            parts.append(lax.ppermute(data, axis_name, [(j, j ^ offset) for j in range(count)]))
        data = jnp.stack(parts)
    return data


def stacked_position(offset, groups):
    position = jnp.zeros_like(offset)
    for group in reversed(groups):
        digit = sum(((offset // bit) % 2) << k for k, bit in enumerate(group))
        position = position * (1 << len(group)) + digit
    return position


def bit_groups(bits):
    return [bits[k : k + 2] for k in range(0, len(bits), 2)]


def gather_operators(x_operator, y_operator, after):
    mem_count = lax.axis_size("mem")
    tile_count = lax.axis_size("tile")
    x_rows, x_cols = x_operator.shape
    y_rows, y_cols = y_operator.shape
    width = max(x_cols, y_cols)
    both = jnp.concatenate(
        [
            jnp.pad(x_operator, ((0, 0), (0, width - x_cols))),
            jnp.pad(y_operator, ((0, 0), (0, width - y_cols))),
        ]
    )
    mem_bits = bit_groups([1 << k for k in range(mem_count.bit_length() - 1)])
    tile_bits = bit_groups([1 << k for k in range(1, tile_count.bit_length() - 1)]) + [[1]]
    both = xor_gather(both, "mem", mem_bits)
    both, after = lax.optimization_barrier((both, after))
    both = xor_gather(both, "tile", tile_bits).reshape(mem_count * tile_count, x_rows + y_rows, width)
    mem_of = lax.broadcasted_iota(jnp.int32, (mem_count, tile_count), 0)
    tile_of = lax.broadcasted_iota(jnp.int32, (mem_count, tile_count), 1)
    position = stacked_position(tile_of ^ lax.axis_index("tile"), tile_bits) * mem_count
    position = position + stacked_position(mem_of ^ lax.axis_index("mem"), mem_bits)
    position = position.reshape(-1)
    x_full = jnp.take(both[:, :x_rows, :x_cols], position, axis=0, mode="clip")
    y_full = jnp.take(both[:, x_rows:, :y_cols], position, axis=0, mode="clip")
    x_full = x_full.reshape(mem_count * tile_count * x_rows, x_cols)
    y_full = y_full.reshape(mem_count * tile_count * y_rows, y_cols)
    return x_full, y_full, after


def body(
    source_blocks, send_blocks, recv_slot, recv_weight, recv_count, regional, x_operator, y_operator
):
    tile_count = lax.axis_size("tile")
    member_count, level_count, columns, y_cells = regional.shape
    capacity = send_blocks.shape[2]
    block_cells = source_blocks.shape[3]
    block_side = math.isqrt(block_cells)
    picked = send_blocks[0].reshape(-1)
    held = source_blocks.shape[0]
    one_hot = (picked[:, None] == lax.broadcasted_iota(jnp.int32, (1, held), 1)).astype(
        source_blocks.dtype
    )
    packed = jnp.dot(
        one_hot, source_blocks.reshape(held, -1), preferred_element_type=jnp.float32
    ).astype(source_blocks.dtype)
    packed = packed.reshape(tile_count, capacity, -1)
    arrived = lax.all_to_all(packed, "tile", split_axis=0, concat_axis=0, tiled=True)
    x_full, y_full, arrived = gather_operators(x_operator, y_operator, arrived)
    slot_count = columns // block_side * (y_cells // block_side)
    live_mask = lax.broadcasted_iota(jnp.int32, (tile_count, capacity), 1) < recv_count[0][:, None]
    weights = jnp.where(live_mask, recv_weight[0], 0.0).reshape(-1)
    slot_match = recv_slot[0].reshape(-1)[None, :] == lax.broadcasted_iota(
        jnp.int32, (slot_count, tile_count * capacity), 0
    )
    remap_weights = jnp.where(slot_match, weights[None, :], 0.0).astype(jnp.bfloat16)
    remapped = jnp.dot(
        remap_weights,
        arrived.reshape(tile_count * capacity, -1),
        preferred_element_type=jnp.float32,
    )
    remapped = remapped.reshape(
        columns // block_side,
        y_cells // block_side,
        member_count,
        level_count,
        block_side,
        block_side,
    )
    remapped = remapped.transpose(2, 3, 0, 4, 1, 5).reshape(
        member_count, level_count, columns, y_cells
    )
    difference = (remapped - regional.astype(jnp.float32)).astype(jnp.bfloat16)
    x_lines = lax.all_to_all(difference, "tile", split_axis=3, concat_axis=2, tiled=True)
    y_chunk = y_cells // tile_count
    lines = x_lines.transpose(2, 0, 1, 3).reshape(tile_count * columns, -1)
    after_first = jnp.dot(x_full, lines, preferred_element_type=jnp.float32).astype(jnp.bfloat16)
    outgoing = after_first.reshape(tile_count, columns, -1)
    tile_back = lax.all_to_all(outgoing, "tile", split_axis=0, concat_axis=0, tiled=True)
    after_second = jnp.einsum(
        "txmly,bty->mlxb",
        tile_back.reshape(tile_count, columns, member_count, level_count, y_chunk),
        y_full.reshape(y_cells, tile_count, y_chunk),
        preferred_element_type=jnp.float32,
    )
    return (regional.astype(jnp.float32) + after_second).astype(jnp.bfloat16)


def solution(mesh):
    placed = (
        P("tile", "mem", None, None),
        P("tile", None, None),
        P("tile", None, None),
        P("tile", None, None),
        P("tile", None),
        P("mem", None, "tile", None),
        P(("mem", "tile"), None),
        P(("mem", "tile"), None),
    )
    return jax.shard_map(
        body, mesh=mesh, in_specs=placed, out_specs=P("mem", None, "tile", None), check_vma=False
    )
```

```python
import math

import jax
import jax.numpy as jnp
from jax import lax
from jax.sharding import PartitionSpec as P


def xor_gather(data, axis_name, groups):
    count = lax.axis_size(axis_name)
    for group in groups:
        parts = [data]
        for code in range(1, 1 << len(group)):
            offset = sum(bit for k, bit in enumerate(group) if code >> k & 1)
            parts.append(lax.ppermute(data, axis_name, [(j, j ^ offset) for j in range(count)]))
        data = jnp.stack(parts)
    return data


def stacked_position(offset, groups):
    position = jnp.zeros_like(offset)
    for group in reversed(groups):
        digit = sum(((offset // bit) % 2) << k for k, bit in enumerate(group))
        position = position * (1 << len(group)) + digit
    return position


def bit_groups(bits):
    return [bits[k : k + 2] for k in range(0, len(bits), 2)]


def gather_operators(x_operator, y_operator, after):
    mem_count = lax.axis_size("mem")
    tile_count = lax.axis_size("tile")
    x_rows, x_cols = x_operator.shape
    y_rows, y_cols = y_operator.shape
    width = max(x_cols, y_cols)
    both = jnp.concatenate(
        [
            jnp.pad(x_operator, ((0, 0), (0, width - x_cols))),
            jnp.pad(y_operator, ((0, 0), (0, width - y_cols))),
        ]
    )
    mem_bits = bit_groups([1 << k for k in range(mem_count.bit_length() - 1)])
    tile_bits = bit_groups([1 << k for k in range(1, tile_count.bit_length() - 1)]) + [[1]]
    both, after = lax.optimization_barrier((both, after))
    both = xor_gather(both, "mem", mem_bits)
    both = xor_gather(both, "tile", tile_bits).reshape(mem_count * tile_count, x_rows + y_rows, width)
    mem_of = lax.broadcasted_iota(jnp.int32, (mem_count, tile_count), 0)
    tile_of = lax.broadcasted_iota(jnp.int32, (mem_count, tile_count), 1)
    position = stacked_position(tile_of ^ lax.axis_index("tile"), tile_bits) * mem_count
    position = position + stacked_position(mem_of ^ lax.axis_index("mem"), mem_bits)
    position = position.reshape(-1)
    x_full = jnp.take(both[:, :x_rows, :x_cols], position, axis=0, mode="clip")
    y_full = jnp.take(both[:, x_rows:, :y_cols], position, axis=0, mode="clip")
    x_full = x_full.reshape(mem_count * tile_count * x_rows, x_cols)
    y_full = y_full.reshape(mem_count * tile_count * y_rows, y_cols)
    return x_full, y_full, after


def body(
    source_blocks, send_blocks, recv_slot, recv_weight, recv_count, regional, x_operator, y_operator
):
    tile_count = lax.axis_size("tile")
    member_count, level_count, columns, y_cells = regional.shape
    capacity = send_blocks.shape[2]
    block_cells = source_blocks.shape[3]
    block_side = math.isqrt(block_cells)
    picked = send_blocks[0].reshape(-1)
    held = source_blocks.shape[0]
    one_hot = (picked[:, None] == lax.broadcasted_iota(jnp.int32, (1, held), 1)).astype(
        source_blocks.dtype
    )
    packed = jnp.dot(
        one_hot, source_blocks.reshape(held, -1), preferred_element_type=jnp.float32
    ).astype(source_blocks.dtype)
    packed = packed.reshape(tile_count, capacity, -1)
    arrived = lax.all_to_all(packed, "tile", split_axis=0, concat_axis=0, tiled=True)
    x_full, y_full, arrived = gather_operators(x_operator, y_operator, arrived)
    slot_count = columns // block_side * (y_cells // block_side)
    live_mask = lax.broadcasted_iota(jnp.int32, (tile_count, capacity), 1) < recv_count[0][:, None]
    weights = jnp.where(live_mask, recv_weight[0], 0.0).reshape(-1)
    slot_match = recv_slot[0].reshape(-1)[None, :] == lax.broadcasted_iota(
        jnp.int32, (slot_count, tile_count * capacity), 0
    )
    remap_weights = jnp.where(slot_match, weights[None, :], 0.0).astype(jnp.bfloat16)
    remapped = jnp.dot(
        remap_weights,
        arrived.reshape(tile_count * capacity, -1),
        preferred_element_type=jnp.float32,
    )
    remapped = remapped.reshape(
        columns // block_side,
        y_cells // block_side,
        member_count,
        level_count,
        block_side,
        block_side,
    )
    remapped = remapped.transpose(2, 3, 0, 4, 1, 5).reshape(
        member_count, level_count, columns, y_cells
    )
    difference = (remapped - regional.astype(jnp.float32)).astype(jnp.bfloat16)
    x_lines = lax.all_to_all(difference, "tile", split_axis=3, concat_axis=2, tiled=True)
    after_first = jnp.einsum(
        "ax,mlxy->mlay",
        x_full,
        x_lines,
        preferred_element_type=jnp.float32,
    ).astype(jnp.bfloat16)
    y_chunk = y_cells // tile_count
    outgoing = after_first.reshape(
        member_count, level_count, tile_count, columns, y_chunk
    ).transpose(2, 0, 1, 3, 4)
    tile_back = lax.all_to_all(outgoing, "tile", split_axis=0, concat_axis=0, tiled=True)
    after_second = jnp.einsum(
        "tmlxy,bty->mlxb",
        tile_back,
        y_full.reshape(y_cells, tile_count, y_chunk),
        preferred_element_type=jnp.float32,
    )
    return (regional.astype(jnp.float32) + after_second).astype(jnp.bfloat16)


def solution(mesh):
    placed = (
        P("tile", "mem", None, None),
        P("tile", None, None),
        P("tile", None, None),
        P("tile", None, None),
        P("tile", None),
        P("mem", None, "tile", None),
        P(("mem", "tile"), None),
        P(("mem", "tile"), None),
    )
    return jax.shard_map(
        body, mesh=mesh, in_specs=placed, out_specs=P("mem", None, "tile", None), check_vma=False
    )
```

```python
import math

import jax
import jax.numpy as jnp
from jax import lax
from jax.sharding import PartitionSpec as P


def xor_gather(data, axis_name, groups):
    count = lax.axis_size(axis_name)
    for group in groups:
        parts = [data]
        for code in range(1, 1 << len(group)):
            offset = sum(bit for k, bit in enumerate(group) if code >> k & 1)
            parts.append(lax.ppermute(data, axis_name, [(j, j ^ offset) for j in range(count)]))
        data = jnp.stack(parts)
    return data


def stacked_position(offset, groups):
    position = jnp.zeros_like(offset)
    for group in reversed(groups):
        digit = sum(((offset // bit) % 2) << k for k, bit in enumerate(group))
        position = position * (1 << len(group)) + digit
    return position


def bit_groups(bits):
    return [bits[k : k + 2] for k in range(0, len(bits), 2)]


def gather_operators(x_operator, y_operator, after):
    mem_count = lax.axis_size("mem")
    tile_count = lax.axis_size("tile")
    x_rows, x_cols = x_operator.shape
    y_rows, y_cols = y_operator.shape
    width = max(x_cols, y_cols)
    both = jnp.concatenate(
        [
            jnp.pad(x_operator, ((0, 0), (0, width - x_cols))),
            jnp.pad(y_operator, ((0, 0), (0, width - y_cols))),
        ]
    )
    mem_bits = bit_groups([1 << k for k in range(mem_count.bit_length() - 1)])
    tile_bits = bit_groups([1 << k for k in range(1, tile_count.bit_length() - 1)]) + [[1]]
    both = xor_gather(both, "mem", mem_bits)
    both, after = lax.optimization_barrier((both, after))
    both = xor_gather(both, "tile", tile_bits).reshape(mem_count * tile_count, x_rows + y_rows, width)
    mem_of = lax.broadcasted_iota(jnp.int32, (mem_count, tile_count), 0)
    tile_of = lax.broadcasted_iota(jnp.int32, (mem_count, tile_count), 1)
    position = stacked_position(tile_of ^ lax.axis_index("tile"), tile_bits) * mem_count
    position = position + stacked_position(mem_of ^ lax.axis_index("mem"), mem_bits)
    position = position.reshape(-1)
    x_full = jnp.take(both[:, :x_rows, :x_cols], position, axis=0, mode="clip")
    y_full = jnp.take(both[:, x_rows:, :y_cols], position, axis=0, mode="clip")
    x_full = x_full.reshape(mem_count * tile_count * x_rows, x_cols)
    y_full = y_full.reshape(mem_count * tile_count * y_rows, y_cols)
    return x_full, y_full, after


def body(
    source_blocks, send_blocks, recv_slot, recv_weight, recv_count, regional, x_operator, y_operator
):
    tile_count = lax.axis_size("tile")
    member_count, level_count, columns, y_cells = regional.shape
    capacity = send_blocks.shape[2]
    block_cells = source_blocks.shape[3]
    block_side = math.isqrt(block_cells)
    order = jnp.arange(tile_count, dtype=jnp.int32) ^ lax.axis_index("tile")
    picked = jnp.take(send_blocks[0], order, axis=0, mode="clip").reshape(-1)
    held = source_blocks.shape[0]
    one_hot = (picked[:, None] == lax.broadcasted_iota(jnp.int32, (1, held), 1)).astype(
        source_blocks.dtype
    )
    packed = jnp.dot(
        one_hot, source_blocks.reshape(held, -1), preferred_element_type=jnp.float32
    ).astype(source_blocks.dtype)
    packed = packed.reshape(tile_count, capacity, -1)
    outgoing = packed
    arrived = jnp.stack(
        [outgoing[0]]
        + [
            lax.ppermute(outgoing[o], "tile", [(j, j ^ o) for j in range(tile_count)])
            for o in range(1, tile_count)
        ]
    )
    x_full, y_full, arrived = gather_operators(x_operator, y_operator, arrived)
    slot_count = columns // block_side * (y_cells // block_side)
    count_of = jnp.take(recv_count[0], order, axis=0, mode="clip")
    weight_of = jnp.take(recv_weight[0], order, axis=0, mode="clip")
    slot_of = jnp.take(recv_slot[0], order, axis=0, mode="clip")
    live_mask = lax.broadcasted_iota(jnp.int32, (tile_count, capacity), 1) < count_of[:, None]
    weights = jnp.where(live_mask, weight_of, 0.0).reshape(-1)
    slot_match = slot_of.reshape(-1)[None, :] == lax.broadcasted_iota(
        jnp.int32, (slot_count, tile_count * capacity), 0
    )
    remap_weights = jnp.where(slot_match, weights[None, :], 0.0).astype(jnp.bfloat16)
    remapped = jnp.dot(
        remap_weights,
        arrived.reshape(tile_count * capacity, -1),
        preferred_element_type=jnp.float32,
    )
    remapped = remapped.reshape(
        columns // block_side,
        y_cells // block_side,
        member_count,
        level_count,
        block_side,
        block_side,
    )
    remapped = remapped.transpose(2, 3, 0, 4, 1, 5).reshape(
        member_count, level_count, columns, y_cells
    )
    difference = (remapped - regional.astype(jnp.float32)).astype(jnp.bfloat16)
    x_lines = lax.all_to_all(difference, "tile", split_axis=3, concat_axis=2, tiled=True)
    after_first = jnp.einsum(
        "ax,mlxy->mlay",
        x_full,
        x_lines,
        preferred_element_type=jnp.float32,
    ).astype(jnp.bfloat16)
    y_chunk = y_cells // tile_count
    outgoing = after_first.reshape(
        member_count, level_count, tile_count, columns, y_chunk
    ).transpose(2, 0, 1, 3, 4)
    tile_back = lax.all_to_all(outgoing, "tile", split_axis=0, concat_axis=0, tiled=True)
    after_second = jnp.einsum(
        "tmlxy,bty->mlxb",
        tile_back,
        y_full.reshape(y_cells, tile_count, y_chunk),
        preferred_element_type=jnp.float32,
    )
    return (regional.astype(jnp.float32) + after_second).astype(jnp.bfloat16)


def solution(mesh):
    placed = (
        P("tile", "mem", None, None),
        P("tile", None, None),
        P("tile", None, None),
        P("tile", None, None),
        P("tile", None),
        P("mem", None, "tile", None),
        P(("mem", "tile"), None),
        P(("mem", "tile"), None),
    )
    return jax.shard_map(
        body, mesh=mesh, in_specs=placed, out_specs=P("mem", None, "tile", None), check_vma=False
    )
```

```python
import math

import jax
import jax.numpy as jnp
from jax import lax
from jax.sharding import PartitionSpec as P


def xor_gather(data, axis_name, groups):
    count = lax.axis_size(axis_name)
    for group in groups:
        parts = [data]
        for code in range(1, 1 << len(group)):
            offset = sum(bit for k, bit in enumerate(group) if code >> k & 1)
            parts.append(lax.ppermute(data, axis_name, [(j, j ^ offset) for j in range(count)]))
        data = jnp.stack(parts)
    return data


def xor_parts(data, axis_name, group):
    count = lax.axis_size(axis_name)
    parts = [data]
    for code in range(1, 1 << len(group)):
        offset = sum(bit for k, bit in enumerate(group) if code >> k & 1)
        parts.append(lax.ppermute(data, axis_name, [(j, j ^ offset) for j in range(count)]))
    return parts


def stacked_position(offset, groups):
    position = jnp.zeros_like(offset)
    for group in reversed(groups):
        digit = sum(((offset // bit) % 2) << k for k, bit in enumerate(group))
        position = position * (1 << len(group)) + digit
    return position


def bit_groups(bits):
    return [bits[k : k + 2] for k in range(0, len(bits), 2)]


def gather_operators(x_operator, y_operator, after):
    mem_count = lax.axis_size("mem")
    tile_count = lax.axis_size("tile")
    x_rows, x_cols = x_operator.shape
    y_rows, y_cols = y_operator.shape
    width = max(x_cols, y_cols)
    both = jnp.concatenate(
        [
            jnp.pad(x_operator, ((0, 0), (0, width - x_cols))),
            jnp.pad(y_operator, ((0, 0), (0, width - y_cols))),
        ]
    )
    mem_bits = bit_groups([1 << k for k in range(mem_count.bit_length() - 1)])
    tile_bits = bit_groups([1 << k for k in range(1, tile_count.bit_length() - 1)]) + [[1]]
    both = xor_gather(both, "mem", mem_bits)
    both, after = lax.optimization_barrier((both, after))
    chip_groups = tile_bits[:-1]
    both = xor_gather(both, "tile", chip_groups[:-1])
    parts = xor_parts(both, "tile", chip_groups[-1]) if chip_groups else [both]
    swapped = [lax.ppermute(part, "tile", [(j, j ^ 1) for j in range(tile_count)]) for part in parts]
    both = jnp.stack([jnp.stack(parts), jnp.stack(swapped)])
    both = both.reshape(mem_count * tile_count, x_rows + y_rows, width)
    mem_of = lax.broadcasted_iota(jnp.int32, (mem_count, tile_count), 0)
    tile_of = lax.broadcasted_iota(jnp.int32, (mem_count, tile_count), 1)
    position = stacked_position(tile_of ^ lax.axis_index("tile"), tile_bits) * mem_count
    position = position + stacked_position(mem_of ^ lax.axis_index("mem"), mem_bits)
    position = position.reshape(-1)
    x_full = jnp.take(both[:, :x_rows, :x_cols], position, axis=0, mode="clip")
    y_full = jnp.take(both[:, x_rows:, :y_cols], position, axis=0, mode="clip")
    x_full = x_full.reshape(mem_count * tile_count * x_rows, x_cols)
    y_full = y_full.reshape(mem_count * tile_count * y_rows, y_cols)
    return x_full, y_full, after


def body(
    source_blocks, send_blocks, recv_slot, recv_weight, recv_count, regional, x_operator, y_operator
):
    tile_count = lax.axis_size("tile")
    member_count, level_count, columns, y_cells = regional.shape
    capacity = send_blocks.shape[2]
    block_cells = source_blocks.shape[3]
    block_side = math.isqrt(block_cells)
    picked = send_blocks[0].reshape(-1)
    held = source_blocks.shape[0]
    one_hot = (picked[:, None] == lax.broadcasted_iota(jnp.int32, (1, held), 1)).astype(
        source_blocks.dtype
    )
    packed = jnp.dot(
        one_hot, source_blocks.reshape(held, -1), preferred_element_type=jnp.float32
    ).astype(source_blocks.dtype)
    packed = packed.reshape(tile_count, capacity, -1)
    arrived = lax.all_to_all(packed, "tile", split_axis=0, concat_axis=0, tiled=True)
    x_full, y_full, arrived = gather_operators(x_operator, y_operator, arrived)
    slot_count = columns // block_side * (y_cells // block_side)
    live_mask = lax.broadcasted_iota(jnp.int32, (tile_count, capacity), 1) < recv_count[0][:, None]
    weights = jnp.where(live_mask, recv_weight[0], 0.0).reshape(-1)
    slot_match = recv_slot[0].reshape(-1)[None, :] == lax.broadcasted_iota(
        jnp.int32, (slot_count, tile_count * capacity), 0
    )
    remap_weights = jnp.where(slot_match, weights[None, :], 0.0).astype(jnp.bfloat16)
    remapped = jnp.dot(
        remap_weights,
        arrived.reshape(tile_count * capacity, -1),
        preferred_element_type=jnp.float32,
    )
    remapped = remapped.reshape(
        columns // block_side,
        y_cells // block_side,
        member_count,
        level_count,
        block_side,
        block_side,
    )
    remapped = remapped.transpose(2, 3, 0, 4, 1, 5).reshape(
        member_count, level_count, columns, y_cells
    )
    difference = (remapped - regional.astype(jnp.float32)).astype(jnp.bfloat16)
    x_lines = lax.all_to_all(difference, "tile", split_axis=3, concat_axis=2, tiled=True)
    after_first = jnp.einsum(
        "ax,mlxy->mlay",
        x_full,
        x_lines,
        preferred_element_type=jnp.float32,
    ).astype(jnp.bfloat16)
    y_chunk = y_cells // tile_count
    outgoing = after_first.reshape(
        member_count, level_count, tile_count, columns, y_chunk
    ).transpose(2, 0, 1, 3, 4)
    tile_back = lax.all_to_all(outgoing, "tile", split_axis=0, concat_axis=0, tiled=True)
    after_second = jnp.einsum(
        "tmlxy,bty->mlxb",
        tile_back,
        y_full.reshape(y_cells, tile_count, y_chunk),
        preferred_element_type=jnp.float32,
    )
    return (regional.astype(jnp.float32) + after_second).astype(jnp.bfloat16)


def solution(mesh):
    placed = (
        P("tile", "mem", None, None),
        P("tile", None, None),
        P("tile", None, None),
        P("tile", None, None),
        P("tile", None),
        P("mem", None, "tile", None),
        P(("mem", "tile"), None),
        P(("mem", "tile"), None),
    )
    return jax.shard_map(
        body, mesh=mesh, in_specs=placed, out_specs=P("mem", None, "tile", None), check_vma=False
    )
```

```python
import math

import jax
import jax.numpy as jnp
from jax import lax
from jax.sharding import PartitionSpec as P


def xor_gather(data, axis_name, groups):
    count = lax.axis_size(axis_name)
    for group in groups:
        parts = [data]
        for code in range(1, 1 << len(group)):
            offset = sum(bit for k, bit in enumerate(group) if code >> k & 1)
            parts.append(lax.ppermute(data, axis_name, [(j, j ^ offset) for j in range(count)]))
        data = jnp.stack(parts)
    return data


def xor_parts(data, axis_name, group):
    count = lax.axis_size(axis_name)
    parts = [data]
    for code in range(1, 1 << len(group)):
        offset = sum(bit for k, bit in enumerate(group) if code >> k & 1)
        parts.append(lax.ppermute(data, axis_name, [(j, j ^ offset) for j in range(count)]))
    return parts


def stacked_position(offset, groups):
    position = jnp.zeros_like(offset)
    for group in reversed(groups):
        digit = sum(((offset // bit) % 2) << k for k, bit in enumerate(group))
        position = position * (1 << len(group)) + digit
    return position


def bit_groups(bits):
    return [bits[k : k + 2] for k in range(0, len(bits), 2)]


def gather_operators(x_operator, y_operator, after):
    mem_count = lax.axis_size("mem")
    tile_count = lax.axis_size("tile")
    x_rows, x_cols = x_operator.shape
    y_rows, y_cols = y_operator.shape
    width = max(x_cols, y_cols)
    both = jnp.concatenate(
        [
            jnp.pad(x_operator, ((0, 0), (0, width - x_cols))),
            jnp.pad(y_operator, ((0, 0), (0, width - y_cols))),
        ]
    )
    mem_bits = bit_groups([1 << k for k in range(mem_count.bit_length() - 1)])
    tile_bits = bit_groups([1 << k for k in range(1, tile_count.bit_length() - 1)]) + [[1]]
    both = xor_gather(both, "mem", mem_bits)
    chip_groups = tile_bits[:-1]
    both = xor_gather(both, "tile", chip_groups[:-1])
    parts = xor_parts(both, "tile", chip_groups[-1]) if chip_groups else [both]
    parts, after = lax.optimization_barrier((parts, after))
    swapped = [lax.ppermute(part, "tile", [(j, j ^ 1) for j in range(tile_count)]) for part in parts]
    both = jnp.stack([jnp.stack(parts), jnp.stack(swapped)])
    both = both.reshape(mem_count * tile_count, x_rows + y_rows, width)
    mem_of = lax.broadcasted_iota(jnp.int32, (mem_count, tile_count), 0)
    tile_of = lax.broadcasted_iota(jnp.int32, (mem_count, tile_count), 1)
    position = stacked_position(tile_of ^ lax.axis_index("tile"), tile_bits) * mem_count
    position = position + stacked_position(mem_of ^ lax.axis_index("mem"), mem_bits)
    position = position.reshape(-1)
    x_full = jnp.take(both[:, :x_rows, :x_cols], position, axis=0, mode="clip")
    y_full = jnp.take(both[:, x_rows:, :y_cols], position, axis=0, mode="clip")
    x_full = x_full.reshape(mem_count * tile_count * x_rows, x_cols)
    y_full = y_full.reshape(mem_count * tile_count * y_rows, y_cols)
    return x_full, y_full, after


def body(
    source_blocks, send_blocks, recv_slot, recv_weight, recv_count, regional, x_operator, y_operator
):
    tile_count = lax.axis_size("tile")
    member_count, level_count, columns, y_cells = regional.shape
    capacity = send_blocks.shape[2]
    block_cells = source_blocks.shape[3]
    block_side = math.isqrt(block_cells)
    picked = send_blocks[0].reshape(-1)
    held = source_blocks.shape[0]
    one_hot = (picked[:, None] == lax.broadcasted_iota(jnp.int32, (1, held), 1)).astype(
        source_blocks.dtype
    )
    packed = jnp.dot(
        one_hot, source_blocks.reshape(held, -1), preferred_element_type=jnp.float32
    ).astype(source_blocks.dtype)
    packed = packed.reshape(tile_count, capacity, -1)
    arrived = lax.all_to_all(packed, "tile", split_axis=0, concat_axis=0, tiled=True)
    slot_count = columns // block_side * (y_cells // block_side)
    live_mask = lax.broadcasted_iota(jnp.int32, (tile_count, capacity), 1) < recv_count[0][:, None]
    weights = jnp.where(live_mask, recv_weight[0], 0.0).reshape(-1)
    slot_match = recv_slot[0].reshape(-1)[None, :] == lax.broadcasted_iota(
        jnp.int32, (slot_count, tile_count * capacity), 0
    )
    remap_weights = jnp.where(slot_match, weights[None, :], 0.0).astype(jnp.bfloat16)
    remapped = jnp.dot(
        remap_weights,
        arrived.reshape(tile_count * capacity, -1),
        preferred_element_type=jnp.float32,
    )
    remapped = remapped.reshape(
        columns // block_side,
        y_cells // block_side,
        member_count,
        level_count,
        block_side,
        block_side,
    )
    remapped = remapped.transpose(2, 3, 0, 4, 1, 5).reshape(
        member_count, level_count, columns, y_cells
    )
    difference = (remapped - regional.astype(jnp.float32)).astype(jnp.bfloat16)
    x_full, y_full, difference = gather_operators(x_operator, y_operator, difference)
    x_lines = lax.all_to_all(difference, "tile", split_axis=3, concat_axis=2, tiled=True)
    after_first = jnp.einsum(
        "ax,mlxy->mlay",
        x_full,
        x_lines,
        preferred_element_type=jnp.float32,
    ).astype(jnp.bfloat16)
    y_chunk = y_cells // tile_count
    outgoing = after_first.reshape(
        member_count, level_count, tile_count, columns, y_chunk
    ).transpose(2, 0, 1, 3, 4)
    tile_back = lax.all_to_all(outgoing, "tile", split_axis=0, concat_axis=0, tiled=True)
    after_second = jnp.einsum(
        "tmlxy,bty->mlxb",
        tile_back,
        y_full.reshape(y_cells, tile_count, y_chunk),
        preferred_element_type=jnp.float32,
    )
    return (regional.astype(jnp.float32) + after_second).astype(jnp.bfloat16)


def solution(mesh):
    placed = (
        P("tile", "mem", None, None),
        P("tile", None, None),
        P("tile", None, None),
        P("tile", None, None),
        P("tile", None),
        P("mem", None, "tile", None),
        P(("mem", "tile"), None),
        P(("mem", "tile"), None),
    )
    return jax.shard_map(
        body, mesh=mesh, in_specs=placed, out_specs=P("mem", None, "tile", None), check_vma=False
    )
```
